32 devices in a mesh: cache: 8 (over z, x), stream: 4 (over y, core).
Axes of the slice: x: 2, y: 2, z: 4, core: 2. Of those that a mesh axis runs over, the one named last changes fastest.
Arguments:
- queries: bfloat16 [2048, 4096], P('cache', 'stream'), may hold values from -12.5 to 12.5
- own_kv: bfloat16 [2048, 1024], P('cache', 'stream'), may hold values from -6 to 6
- passage_store: bfloat16 [128, 512, 1024], P('cache', None, 'stream'), may hold values from -6 to 6
- out_weight: bfloat16 [4096, 8192], P('stream', 'cache'), may hold values from -0.375 to 0.375
- passage_slot: int32 [128], replicated, may hold values from 0 to 127, as said below
- retrieved: int32 [16, 16], P('cache'), may hold values from 0 to 127, as said below
Outputs:
- layer_out: bfloat16 [2048, 8192], P('cache', 'stream')
The draws below stay inside these ranges and needn't reach their ends.
Inputs may be any that keep to these rules, and one draw needn't show every extreme that they name: `passage_slot`: a permutation. `retrieved`: over the 2 queries of one index of cache all ids are distinct; at most 8 of their slots fall in any one block of 16 consecutive slots, and some block holds exactly 8 of them for every index of cache.
All inputs are finite; a program needn't handle non-finite values.
Results may differ from the reference program's by a relative error of at most 0.015.
Values may be sent and summed in bfloat16 or wider, within the bound.
No kernel may reach another device: no remote copies, remote signals or barrier semaphores. Data moves between devices by JAX's collectives and lax.ppermute only.
A program may use at most 192 MiB of HBM per device.

```python
import math
from functools import partial
import jax
import jax.numpy as jnp
from jax import lax

D = 8192
HQ = 32
KVH = 4
HD = 128
QLEN = 128
PLEN = 512
K_RET = 16
Q_DEV = 2
P_DEV = 16
QUERIES = 16
TOKENS = 2048
P_TOTAL = 128
REQ = 32
CAP = 8


def id_at_slot(key):
    return jax.random.permutation(jax.random.fold_in(key, 3), P_TOTAL).astype(jnp.int32)


def draw_passage_slot(key, part):
    return jnp.argsort(id_at_slot(key)).astype(jnp.int32)


def device_requests(key, ids_by_slot, hot_owner, device):
    sub_key = jax.random.fold_in(key, 1000 + device)
    owner_total = P_TOTAL // P_DEV
    slot_total = owner_total * CAP
    shuffle = jax.random.permutation(jax.random.fold_in(sub_key, 1), slot_total).astype(jnp.int32)
    owner_of = shuffle // CAP
    first_owner = owner_of[0]
    places = jnp.arange(slot_total, dtype=jnp.int32)
    rank_key = places - slot_total * (owner_of == first_owner).astype(jnp.int32) - 2 * slot_total * (owner_of == hot_owner).astype(jnp.int32)
    ordering = jnp.argsort(rank_key)
    chosen = shuffle[ordering[:REQ]]
    chosen = chosen[jax.random.permutation(jax.random.fold_in(sub_key, 2), REQ)]
    owners = chosen // CAP
    spots = jnp.arange(REQ, dtype=jnp.int32)
    earlier = (owners[None, :] == owners[:, None]) & (spots[None, :] < spots[:, None])
    order_rank = jnp.sum(earlier, axis=1).astype(jnp.int32)
    shifts = jax.random.randint(jax.random.fold_in(sub_key, 3), (owner_total,), 0, P_DEV).astype(jnp.int32)
    local_rows = (shifts[owners] + order_rank) % P_DEV
    return ids_by_slot[owners * P_DEV + local_rows]


def draw_retrieved(key, part):
    ids_by_slot = id_at_slot(key)
    hot_owner = jax.random.randint(jax.random.fold_in(key, 5), (), 0, P_TOTAL // P_DEV).astype(jnp.int32)
    devices = jnp.arange(QUERIES // Q_DEV, dtype=jnp.int32)
    rows = jax.vmap(partial(device_requests, key, ids_by_slot, hot_owner))(devices)
    return rows.reshape(QUERIES, K_RET).astype(jnp.int32)


def attention_inputs(key):
    base = jax.random.fold_in(key, 11)
    groups = HQ // KVH
    shape_query = (QUERIES, QLEN, KVH, groups, HD)
    shape_key = (QUERIES, QLEN, KVH, HD)
    direction = jax.random.truncated_normal(jax.random.fold_in(base, 1), -4.0, 4.0, (QUERIES, 1, KVH, 1, HD))
    query_noise = jax.random.truncated_normal(jax.random.fold_in(base, 2), -4.0, 4.0, shape_query)
    key_noise = jax.random.truncated_normal(jax.random.fold_in(base, 3), -4.0, 4.0, shape_key)
    value_noise = jax.random.truncated_normal(jax.random.fold_in(base, 4), -4.0, 4.0, shape_key)
    query_vals = 2.4 * query_noise + 0.7 * direction
    key_vals = 0.8 * key_noise + 0.6 * direction[:, :, :, 0, :]
    value_vals = value_noise
    query_out = query_vals.reshape(TOKENS, HQ * HD)
    own_out = jnp.stack([key_vals, value_vals], axis=3).reshape(TOKENS, KVH * 2 * HD)
    return (query_out, own_out)


def draw_queries(key, part):
    return attention_inputs(key)[0].astype(jnp.float32).astype(jnp.bfloat16)


def draw_own_kv(key, part):
    return attention_inputs(key)[1].astype(jnp.float32).astype(jnp.bfloat16)


def block_scale(rng, shape, cuts, low, high):
    level, own = 1.0, jax.random.fold_in(rng, 6)
    for axis_at, parts in cuts:
        steps = jnp.exp(jax.random.uniform(jax.random.fold_in(own, axis_at), (parts,), jnp.float32, low / len(cuts), high / len(cuts)))
        level = level * jnp.repeat(steps, shape[axis_at] // parts).reshape([-1 if axis == axis_at else 1 for axis in range(len(shape))])
    return level


def noise(rng, extent, deviation, limit, shards=(), held_as=jnp.bfloat16):
    values = deviation * jax.random.normal(rng, extent, jnp.float32)
    if shards:
        values = values * block_scale(rng, extent, shards, -0.22, 0.18)
    return jnp.clip(values, -limit, limit).astype(held_as)


def setup_inputs(seed: int = 0) -> dict:
    streams_of = jax.random.split(jax.random.key(seed), 7)
    return {
        "queries": draw_queries(jax.random.fold_in(streams_of[6], 71), 0),
        "own_kv": draw_own_kv(jax.random.fold_in(streams_of[6], 71), 0),
        "passage_store": noise(streams_of[2], (P_TOTAL, PLEN, KVH * 2 * HD), 1.0, 6.0, ((0, 8), (2, 4))),
        "out_weight": noise(streams_of[3], (HQ * HD, D), (HQ * HD // 16) ** -0.5, 0.375, ((0, 4), (1, 8))),
        "passage_slot": draw_passage_slot(jax.random.fold_in(streams_of[6], 71), 0),
        "retrieved": draw_retrieved(jax.random.fold_in(streams_of[6], 71), 0),
    }


def attend_query(query_rows, own_rows, passages):
    groups = HQ // KVH
    passage_len = K_RET * PLEN
    length = passage_len + QLEN
    context = jnp.concatenate([passages.reshape(passage_len, KVH * 2 * HD), own_rows], axis=0).reshape(length, KVH, 2, HD)
    key_part = context[:, :, 0, :].astype(jnp.float32)
    value_part = context[:, :, 1, :].astype(jnp.float32)
    query_part = query_rows.reshape(QLEN, KVH, groups, HD).astype(jnp.float32)
    scores = jnp.einsum('tkgd,lkd->kgtl', query_part, key_part) / math.sqrt(HD)
    position = jnp.arange(length)[None, :] - passage_len
    visible = position <= jnp.arange(QLEN)[:, None]
    scores = jnp.where(visible, scores, -jnp.inf)
    row_peak = lax.optimization_barrier(jnp.max(scores, axis=-1, keepdims=True))
    powers = jnp.exp(scores - row_peak)
    totals = lax.optimization_barrier(jnp.sum(powers, axis=-1))
    soft_weights = powers.astype(jnp.bfloat16).astype(jnp.float32)
    weighted = jnp.einsum('kgtl,lkd->tkgd', soft_weights, value_part)
    attended = weighted / jnp.transpose(totals, (2, 0, 1))[..., None]
    return attended.reshape(QLEN, HQ * HD).astype(jnp.bfloat16)

def reference(queries, own_kv, passage_store, out_weight, passage_slot, retrieved):
    store_rows = passage_slot[retrieved]

    def per_query(inputs):
        query_rows, own_rows, query_slots = inputs
        return attend_query(query_rows, own_rows, passage_store[query_slots])
    attended = lax.map(per_query, (queries.reshape(QUERIES, QLEN, HQ * HD), own_kv.reshape(QUERIES, QLEN, KVH * 2 * HD), store_rows))
    attended = attended.reshape(TOKENS, HQ * HD)
    return jnp.dot(attended, out_weight, preferred_element_type=jnp.float32).astype(jnp.bfloat16)
```

```python
import math

import jax
import jax.numpy as jnp
from jax import lax
from jax.sharding import PartitionSpec as P

HD = 128
QLEN = 128
PLEN = 512


def attend_query(query_rows, own_rows, passages):
    kv_count = own_rows.shape[1] // (2 * HD)
    groups = query_rows.shape[1] // (kv_count * HD)
    tokens_here = query_rows.shape[0]
    passage_len = passages.shape[0]
    length = passage_len + tokens_here
    context = jnp.concatenate([passages, own_rows], axis=0).reshape(length, kv_count, 2, HD)
    key_part = context[:, :, 0, :]
    value_part = context[:, :, 1, :]
    query_part = query_rows.reshape(tokens_here, kv_count, groups, HD)
    scores = jnp.einsum(
        "tkgd,lkd->kgtl", query_part, key_part, preferred_element_type=jnp.float32
    ) / math.sqrt(HD)
    position = jnp.arange(length)[None, :] - passage_len
    visible = position <= jnp.arange(tokens_here)[:, None]
    scores = jnp.where(visible, scores, -jnp.inf)
    row_peak = jnp.max(scores, axis=-1, keepdims=True)
    powers = jnp.exp(scores - row_peak)
    totals = jnp.sum(powers, axis=-1)
    soft_weights = powers.astype(jnp.bfloat16)
    weighted = jnp.einsum(
        "kgtl,lkd->tkgd", soft_weights, value_part, preferred_element_type=jnp.float32
    )
    attended = weighted / jnp.transpose(totals, (2, 0, 1))[..., None]
    return attended.reshape(tokens_here, kv_count * groups * HD).astype(jnp.bfloat16)


def shards(queries, own_kv, passage_store, out_weight, passage_slot, retrieved):
    n_cache = lax.axis_size("cache")
    store_count = passage_store.shape[0]
    width_kv = passage_store.shape[2]
    slot_total = passage_slot.shape[0]
    query_count, per_query = retrieved.shape
    wanted_count = query_count * per_query
    capacity = max(2, (2 * wanted_count + n_cache - 1) // n_cache)
    wanted = retrieved.reshape(wanted_count)
    id_match = wanted[:, None] == jnp.arange(slot_total, dtype=jnp.int32)[None, :]
    store_slots = jnp.sum(jnp.where(id_match, passage_slot[None, :], 0), axis=1)
    owners = store_slots // store_count
    local_rows = store_slots % store_count
    places = jnp.arange(wanted_count, dtype=jnp.int32)
    earlier = (owners[None, :] == owners[:, None]) & (places[None, :] < places[:, None])
    order_rank = jnp.sum(earlier, axis=1)
    flat_slot = owners * capacity + order_rank
    slot_match = flat_slot[:, None] == jnp.arange(n_cache * capacity, dtype=jnp.int32)[None, :]
    send_rows = jnp.sum(jnp.where(slot_match, local_rows[:, None], 0), axis=0).reshape(
        n_cache, capacity
    )
    asked_rows = lax.all_to_all(send_rows, "cache", split_axis=0, concat_axis=0, tiled=True)
    outgoing = passage_store[asked_rows]
    arrived = lax.all_to_all(outgoing, "cache", split_axis=0, concat_axis=0, tiled=True)
    picked = arrived.reshape(n_cache * capacity, PLEN, width_kv)[flat_slot]

    def per_query_block(inputs):
        query_rows, own_rows, passages = inputs
        return attend_query(query_rows, own_rows, passages)

    attended = lax.map(
        per_query_block,
        (
            queries.reshape(query_count, QLEN, queries.shape[1]),
            own_kv.reshape(query_count, QLEN, own_kv.shape[1]),
            picked.reshape(query_count, per_query * PLEN, width_kv),
        ),
    )
    attended = attended.reshape(query_count * QLEN, queries.shape[1])
    return project(attended, out_weight)


def project(attended, out_weight):
    n_cache = lax.axis_size("cache")
    n_stream = lax.axis_size("stream")
    rows = attended.shape[0]
    group = n_cache // n_stream
    everyone = lax.all_gather(attended, "cache", axis=0, tiled=True)
    partial_sums = jnp.dot(everyone, out_weight, preferred_element_type=jnp.float32)
    reduced = lax.psum_scatter(
        partial_sums.astype(jnp.bfloat16), "stream", scatter_dimension=0, tiled=True
    )
    me = lax.axis_index("cache")
    width = reduced.shape[1]
    out = jnp.zeros((rows, group * width), reduced.dtype)
    for r in range(group):
        take = (me % group + r) % group
        piece = lax.dynamic_slice_in_dim(reduced, take * rows, rows, axis=0)
        perm = []
        for c in range(n_cache):
            for s in range(n_stream):
                dst_c = s * group + (c % group + r) % group
                dst_s = c // group
                perm.append((c * n_stream + s, dst_c * n_stream + dst_s))
        got = lax.ppermute(piece, ("cache", "stream"), perm)
        put = (me - r) % group
        out = lax.dynamic_update_slice_in_dim(out, got, put * width, axis=1)
    return out


def solution(mesh):
    return jax.shard_map(
        shards,
        mesh=mesh,
        in_specs=(
            P("cache", "stream"),
            P("cache", "stream"),
            P("cache", None, "stream"),
            P("stream", "cache"),
            P(),
            P("cache", None),
        ),
        out_specs=P("cache", "stream"),
        check_vma=False,
    )
```

```python
import math

import jax
import jax.numpy as jnp
from jax import lax
from jax.experimental import pallas as pl
from jax.experimental.pallas import tpu as pltpu
from jax.sharding import PartitionSpec as P

HD = 128
QLEN = 128
PLEN = 512
FLOOR = -1e30


def slot_kernel(rows_ref, pick_ref, q_ref, kv_ref, acc_ref, peak_ref, total_ref):
    heads = q_ref.shape[2] // HD
    keys = kv_ref[0, :, 0:HD]
    values = kv_ref[0, :, HD:2 * HD]
    for h in range(heads):
        q = q_ref[0, :, h * HD:(h + 1) * HD]
        s = lax.dot_general(
            q, keys, (((1,), (1,)), ((), ())), preferred_element_type=jnp.float32
        ) / math.sqrt(HD)
        m = jnp.max(s, axis=1, keepdims=True)
        p = jnp.exp(s - m)
        peak_ref[0, h] = m
        total_ref[0, h] = jnp.sum(p, axis=1, keepdims=True)
        acc_ref[0, h] = jnp.dot(
            p.astype(jnp.bfloat16), values, preferred_element_type=jnp.float32
        )


def slot_attention(rows, pick, q_blocks, store):
    n_slots = rows.shape[0]
    width = q_blocks.shape[2]
    heads = width // HD
    flops = n_slots * heads * QLEN * PLEN * HD * 4
    return pl.pallas_call(
        slot_kernel,
        out_shape=(
            jax.ShapeDtypeStruct((n_slots, heads, QLEN, HD), jnp.float32),
            jax.ShapeDtypeStruct((n_slots, heads, QLEN, 1), jnp.float32),
            jax.ShapeDtypeStruct((n_slots, heads, QLEN, 1), jnp.float32),
        ),
        grid_spec=pltpu.PrefetchScalarGridSpec(
            num_scalar_prefetch=2,
            grid=(n_slots,),
            in_specs=[
                pl.BlockSpec((1, QLEN, width), lambda i, r, p: (p[i], 0, 0)),
                pl.BlockSpec((1, PLEN, 2 * HD), lambda i, r, p: (r[i], 0, 0)),
            ],
            out_specs=[
                pl.BlockSpec((1, heads, QLEN, HD), lambda i, r, p: (i, 0, 0, 0)),
                pl.BlockSpec((1, heads, QLEN, 1), lambda i, r, p: (i, 0, 0, 0)),
                pl.BlockSpec((1, heads, QLEN, 1), lambda i, r, p: (i, 0, 0, 0)),
            ],
        ),
        cost_estimate=pl.CostEstimate(
            flops=flops,
            transcendentals=n_slots * heads * QLEN * PLEN,
            bytes_accessed=n_slots * (QLEN * width * 2 + PLEN * 2 * HD * 2 + heads * QLEN * HD * 4),
        ),
    )(rows, pick, q_blocks, store)


def own_part(query_rows, own_rows):
    count, tokens, width = query_rows.shape
    heads = width // HD
    q = query_rows.reshape(count, tokens, heads, HD)
    keys = own_rows[:, :, 0:HD]
    values = own_rows[:, :, HD:2 * HD]
    s = jnp.einsum("qthd,qld->qhtl", q, keys, preferred_element_type=jnp.float32) / math.sqrt(HD)
    visible = jnp.arange(tokens)[None, :] <= jnp.arange(tokens)[:, None]
    s = jnp.where(visible, s, -jnp.inf)
    m = jnp.max(s, axis=-1, keepdims=True)
    p = jnp.exp(s - m)
    total = jnp.sum(p, axis=-1, keepdims=True)
    acc = jnp.einsum(
        "qhtl,qld->qhtd", p.astype(jnp.bfloat16), values, preferred_element_type=jnp.float32
    )
    return acc, m, total


def shards(queries, own_kv, passage_store, out_weight, passage_slot, retrieved):
    n_cache = lax.axis_size("cache")
    store_count = passage_store.shape[0]
    slot_total = passage_slot.shape[0]
    query_count, per_query = retrieved.shape
    width = queries.shape[1]
    heads = width // HD
    wanted_count = query_count * per_query
    capacity = max(2, (2 * wanted_count + n_cache - 1) // n_cache)
    wanted = retrieved.reshape(wanted_count)
    id_match = wanted[:, None] == jnp.arange(slot_total, dtype=jnp.int32)[None, :]
    store_slots = jnp.sum(jnp.where(id_match, passage_slot[None, :], 0), axis=1)
    owners = store_slots // store_count
    local_rows = store_slots % store_count
    places = jnp.arange(wanted_count, dtype=jnp.int32)
    earlier = (owners[None, :] == owners[:, None]) & (places[None, :] < places[:, None])
    order_rank = jnp.sum(earlier, axis=1)
    flat_slot = owners * capacity + order_rank
    slot_match = flat_slot[:, None] == jnp.arange(n_cache * capacity, dtype=jnp.int32)[None, :]
    send_rows = jnp.sum(jnp.where(slot_match, local_rows[:, None], 0), axis=0)
    send_query = jnp.sum(jnp.where(slot_match, (places // per_query)[:, None], 0), axis=0)
    send_valid = jnp.sum(slot_match.astype(jnp.int32), axis=0)
    info = jnp.stack([send_rows, send_query, send_valid], axis=0).reshape(3, n_cache, capacity)
    asked = lax.all_to_all(info, "cache", split_axis=1, concat_axis=1, tiled=True)
    asked_rows = asked[0].reshape(n_cache * capacity)
    asked_query = asked[1]
    asked_valid = asked[2] > 0
    requester = jnp.arange(n_cache, dtype=jnp.int32)[:, None]
    pick = (requester * query_count + asked_query).reshape(n_cache * capacity)

    everyone_q = lax.all_gather(queries, "cache", axis=0, tiled=True)
    q_blocks = everyone_q.reshape(n_cache * query_count, QLEN, width)
    acc, peak, total = slot_attention(asked_rows, pick, q_blocks, passage_store)
    acc = acc.reshape(n_cache, capacity, 1, heads, QLEN, HD)
    peak = peak.reshape(n_cache, capacity, 1, heads, QLEN, 1)
    total = total.reshape(n_cache, capacity, 1, heads, QLEN, 1)
    chosen = asked_valid[:, :, None] & (
        asked_query[:, :, None] == jnp.arange(query_count, dtype=jnp.int32)[None, None, :]
    )
    chosen = chosen[:, :, :, None, None, None]
    merged_peak = jnp.max(jnp.where(chosen, peak, FLOOR), axis=1)
    scale = jnp.where(chosen, jnp.exp(peak - merged_peak[:, None]), 0.0)
    merged_acc = jnp.sum(scale * acc, axis=1)
    merged_total = jnp.sum(scale * total, axis=1)
    stats = jnp.concatenate([merged_peak, merged_total], axis=-1)
    back_acc = lax.all_to_all(
        merged_acc.astype(jnp.bfloat16), "cache", split_axis=0, concat_axis=0, tiled=True
    )
    back_stats = lax.all_to_all(stats, "cache", split_axis=0, concat_axis=0, tiled=True)

    own_acc, own_peak, own_total = own_part(
        queries.reshape(query_count, QLEN, width),
        own_kv.reshape(query_count, QLEN, own_kv.shape[1]),
    )
    far_peak = back_stats[..., 0:1]
    far_total = back_stats[..., 1:2]
    top = jnp.maximum(jnp.max(far_peak, axis=0), own_peak)
    far_scale = jnp.exp(far_peak - top[None])
    own_scale = jnp.exp(own_peak - top)
    numer = jnp.sum(far_scale * back_acc.astype(jnp.float32), axis=0) + own_scale * own_acc
    denom = jnp.sum(far_scale * far_total, axis=0) + own_scale * own_total
    attended = (numer / denom).astype(jnp.bfloat16)
    attended = jnp.transpose(attended, (0, 2, 1, 3)).reshape(query_count * QLEN, width)
    return project(attended, out_weight)


def project(attended, out_weight):
    n_cache = lax.axis_size("cache")
    n_stream = lax.axis_size("stream")
    rows = attended.shape[0]
    group = n_cache // n_stream
    everyone = lax.all_gather(attended, "cache", axis=0, tiled=True)
    partial_sums = jnp.dot(everyone, out_weight, preferred_element_type=jnp.float32)
    reduced = lax.psum_scatter(
        partial_sums.astype(jnp.bfloat16), "stream", scatter_dimension=0, tiled=True
    )
    me = lax.axis_index("cache")
    width = reduced.shape[1]
    out = jnp.zeros((rows, group * width), reduced.dtype)
    for r in range(group):
        take = (me % group + r) % group
        piece = lax.dynamic_slice_in_dim(reduced, take * rows, rows, axis=0)
        perm = []
        for c in range(n_cache):
            for s in range(n_stream):
                dst_c = s * group + (c % group + r) % group
                dst_s = c // group
                perm.append((c * n_stream + s, dst_c * n_stream + dst_s))
        got = lax.ppermute(piece, ("cache", "stream"), perm)
        put = (me - r) % group
        out = lax.dynamic_update_slice_in_dim(out, got, put * width, axis=1)
    return out


def solution(mesh):
    return jax.shard_map(
        shards,
        mesh=mesh,
        in_specs=(
            P("cache", "stream"),
            P("cache", "stream"),
            P("cache", None, "stream"),
            P("stream", "cache"),
            P(),
            P("cache", None),
        ),
        out_specs=P("cache", "stream"),
        check_vma=False,
    )
```

```python
import math

import jax
import jax.numpy as jnp
from jax import lax
from jax.experimental import pallas as pl
from jax.experimental.pallas import tpu as pltpu
from jax.sharding import PartitionSpec as P

HD = 128
QLEN = 128
PLEN = 512
FLOOR = -1e30


def slot_kernel(rows_ref, pick_ref, valid_ref, which_ref, q_ref, kv_ref,
                acc_out, peak_out, total_out, acc_sc, peak_sc, total_sc):
    r = pl.program_id(0)
    k = pl.program_id(1)
    cap = pl.num_programs(1)
    heads = q_ref.shape[2] // HD

    @pl.when(k == 0)
    def _():
        acc_sc[...] = jnp.zeros_like(acc_sc)
        peak_sc[...] = jnp.full_like(peak_sc, FLOOR)
        total_sc[...] = jnp.zeros_like(total_sc)

    i = r * cap + k

    @pl.when(valid_ref[i] > 0)
    def _():
        j = which_ref[i]
        keys = kv_ref[0, :, 0:HD]
        values = kv_ref[0, :, HD:2 * HD]
        q = jnp.concatenate([q_ref[0, :, h * HD:(h + 1) * HD] for h in range(heads)], axis=0)
        s = lax.dot_general(
            q, keys, (((1,), (1,)), ((), ())), preferred_element_type=jnp.float32
        ) * (1.0 / math.sqrt(HD))
        old = peak_sc[j]
        new = jnp.maximum(old, jnp.max(s, axis=1, keepdims=True))
        fade = jnp.exp(old - new)
        p = jnp.exp(s - new)
        total_sc[j] = fade * total_sc[j] + jnp.sum(p, axis=1, keepdims=True)
        acc_sc[j] = fade * acc_sc[j] + jnp.dot(
            p.astype(jnp.bfloat16), values, preferred_element_type=jnp.float32
        )
        peak_sc[j] = new

    @pl.when(k == cap - 1)
    def _():
        acc_out[0] = acc_sc[...].astype(acc_out.dtype)
        peak_out[0] = peak_sc[...]
        total_out[0] = total_sc[...]


def slot_attention(rows, pick, valid, which, q_blocks, store, n_req, cap, n_query):
    width = q_blocks.shape[2]
    heads = width // HD
    n_slots = n_req * cap
    stacked = heads * QLEN
    flops = n_slots * heads * QLEN * PLEN * HD * 4
    return pl.pallas_call(
        slot_kernel,
        out_shape=(
            jax.ShapeDtypeStruct((n_req, n_query, stacked, HD), jnp.bfloat16),
            jax.ShapeDtypeStruct((n_req, n_query, stacked, 1), jnp.float32),
            jax.ShapeDtypeStruct((n_req, n_query, stacked, 1), jnp.float32),
        ),
        grid_spec=pltpu.PrefetchScalarGridSpec(
            num_scalar_prefetch=4,
            grid=(n_req, cap),
            in_specs=[
                pl.BlockSpec((1, QLEN, width), lambda r, k, rw, pk, vd, wh: (pk[r * cap + k], 0, 0)),
                pl.BlockSpec((1, PLEN, 2 * HD), lambda r, k, rw, pk, vd, wh: (rw[r * cap + k], 0, 0)),
            ],
            out_specs=[
                pl.BlockSpec((1, n_query, stacked, HD), lambda r, k, rw, pk, vd, wh: (r, 0, 0, 0)),
                pl.BlockSpec((1, n_query, stacked, 1), lambda r, k, rw, pk, vd, wh: (r, 0, 0, 0)),
                pl.BlockSpec((1, n_query, stacked, 1), lambda r, k, rw, pk, vd, wh: (r, 0, 0, 0)),
            ],
            scratch_shapes=[
                pltpu.VMEM((n_query, stacked, HD), jnp.float32),
                pltpu.VMEM((n_query, stacked, 1), jnp.float32),
                pltpu.VMEM((n_query, stacked, 1), jnp.float32),
            ],
        ),
        cost_estimate=pl.CostEstimate(
            flops=flops,
            transcendentals=n_slots * heads * QLEN * PLEN,
            bytes_accessed=n_slots * (QLEN * width * 2 + PLEN * 2 * HD * 2)
            + n_req * n_query * stacked * HD * 2,
        ),
    )(rows, pick, valid, which, q_blocks, store)


def own_part(query_rows, own_rows):
    count, tokens, width = query_rows.shape
    heads = width // HD
    q = query_rows.reshape(count, tokens, heads, HD)
    keys = own_rows[:, :, 0:HD]
    values = own_rows[:, :, HD:2 * HD]
    s = jnp.einsum("qthd,qld->qhtl", q, keys, preferred_element_type=jnp.float32) / math.sqrt(HD)
    visible = jnp.arange(tokens)[None, :] <= jnp.arange(tokens)[:, None]
    s = jnp.where(visible, s, -jnp.inf)
    m = jnp.max(s, axis=-1, keepdims=True)
    p = jnp.exp(s - m)
    total = jnp.sum(p, axis=-1, keepdims=True)
    acc = jnp.einsum(
        "qhtl,qld->qhtd", p.astype(jnp.bfloat16), values, preferred_element_type=jnp.float32
    )
    return acc, m, total


def shards(queries, own_kv, passage_store, out_weight, passage_slot, retrieved):
    n_cache = lax.axis_size("cache")
    store_count = passage_store.shape[0]
    slot_total = passage_slot.shape[0]
    query_count, per_query = retrieved.shape
    width = queries.shape[1]
    heads = width // HD
    wanted_count = query_count * per_query
    capacity = max(2, (2 * wanted_count + n_cache - 1) // n_cache)
    wanted = retrieved.reshape(wanted_count)
    id_match = wanted[:, None] == jnp.arange(slot_total, dtype=jnp.int32)[None, :]
    store_slots = jnp.sum(jnp.where(id_match, passage_slot[None, :], 0), axis=1)
    owners = store_slots // store_count
    local_rows = store_slots % store_count
    places = jnp.arange(wanted_count, dtype=jnp.int32)
    earlier = (owners[None, :] == owners[:, None]) & (places[None, :] < places[:, None])
    order_rank = jnp.sum(earlier, axis=1)
    flat_slot = owners * capacity + order_rank
    slot_match = flat_slot[:, None] == jnp.arange(n_cache * capacity, dtype=jnp.int32)[None, :]
    send_rows = jnp.sum(jnp.where(slot_match, local_rows[:, None], 0), axis=0)
    send_query = jnp.sum(jnp.where(slot_match, (places // per_query)[:, None], 0), axis=0)
    send_valid = jnp.sum(slot_match.astype(jnp.int32), axis=0)
    info = jnp.stack([send_rows, send_query, send_valid], axis=0).reshape(3, n_cache, capacity)
    asked = lax.all_to_all(info, "cache", split_axis=1, concat_axis=1, tiled=True)
    asked_rows = asked[0].reshape(n_cache * capacity)
    asked_query = asked[1]
    requester = jnp.arange(n_cache, dtype=jnp.int32)[:, None]
    pick = (requester * query_count + asked_query).reshape(n_cache * capacity)

    everyone_q = lax.all_gather(queries, "cache", axis=0, tiled=True)
    q_blocks = everyone_q.reshape(n_cache * query_count, QLEN, width)
    merged_acc, merged_peak, merged_total = slot_attention(
        asked_rows, pick, asked[2].reshape(n_cache * capacity), asked_query.reshape(n_cache * capacity),
        q_blocks, passage_store, n_cache, capacity, query_count,
    )
    merged_acc = merged_acc.reshape(n_cache, query_count, heads, QLEN, HD)
    stats = jnp.concatenate([merged_peak, merged_total], axis=-1).reshape(
        n_cache, query_count, heads, QLEN, 2
    )
    back_acc = lax.all_to_all(
        merged_acc, "cache", split_axis=0, concat_axis=0, tiled=True
    )
    back_stats = lax.all_to_all(stats, "cache", split_axis=0, concat_axis=0, tiled=True)

    own_acc, own_peak, own_total = own_part(
        queries.reshape(query_count, QLEN, width),
        own_kv.reshape(query_count, QLEN, own_kv.shape[1]),
    )
    far_peak = back_stats[..., 0:1]
    far_total = back_stats[..., 1:2]
    top = jnp.maximum(jnp.max(far_peak, axis=0), own_peak)
    far_scale = jnp.exp(far_peak - top[None])
    own_scale = jnp.exp(own_peak - top)
    numer = jnp.sum(far_scale * back_acc.astype(jnp.float32), axis=0) + own_scale * own_acc
    denom = jnp.sum(far_scale * far_total, axis=0) + own_scale * own_total
    attended = (numer / denom).astype(jnp.bfloat16)
    attended = jnp.transpose(attended, (0, 2, 1, 3)).reshape(query_count * QLEN, width)
    return project(attended, out_weight)


def project(attended, out_weight):
    n_cache = lax.axis_size("cache")
    n_stream = lax.axis_size("stream")
    rows = attended.shape[0]
    group = n_cache // n_stream
    everyone = lax.all_gather(attended, "cache", axis=0, tiled=True)
    partial_sums = jnp.dot(everyone, out_weight, preferred_element_type=jnp.float32)
    reduced = lax.psum_scatter(
        partial_sums.astype(jnp.bfloat16), "stream", scatter_dimension=0, tiled=True
    )
    me = lax.axis_index("cache")
    width = reduced.shape[1]
    out = jnp.zeros((rows, group * width), reduced.dtype)
    for r in range(group):
        take = (me % group + r) % group
        piece = lax.dynamic_slice_in_dim(reduced, take * rows, rows, axis=0)
        perm = []
        for c in range(n_cache):
            for s in range(n_stream):
                dst_c = s * group + (c % group + r) % group
                dst_s = c // group
                perm.append((c * n_stream + s, dst_c * n_stream + dst_s))
        got = lax.ppermute(piece, ("cache", "stream"), perm)
        put = (me - r) % group
        out = lax.dynamic_update_slice_in_dim(out, got, put * width, axis=1)
    return out


def solution(mesh):
    return jax.shard_map(
        shards,
        mesh=mesh,
        in_specs=(
            P("cache", "stream"),
            P("cache", "stream"),
            P("cache", None, "stream"),
            P("stream", "cache"),
            P(),
            P("cache", None),
        ),
        out_specs=P("cache", "stream"),
        check_vma=False,
    )
```

```python
import math

import jax
import jax.numpy as jnp
from jax import lax
from jax.experimental import pallas as pl
from jax.experimental.pallas import tpu as pltpu
from jax.sharding import PartitionSpec as P

HD = 128
QLEN = 128
PLEN = 512
FLOOR = -1e30


def slot_kernel(rows_ref, pick_ref, valid_ref, which_ref, q_ref, kv_ref,
                acc_out, peak_out, total_out, acc_sc, peak_sc, total_sc):
    r = pl.program_id(0)
    k = pl.program_id(1)
    cap = pl.num_programs(1)
    heads = q_ref.shape[2] // HD

    @pl.when(k == 0)
    def _():
        acc_sc[...] = jnp.zeros_like(acc_sc)
        peak_sc[...] = jnp.full_like(peak_sc, FLOOR)
        total_sc[...] = jnp.zeros_like(total_sc)

    i = r * cap + k

    @pl.when(valid_ref[i] > 0)
    def _():
        j = which_ref[i]
        keys = kv_ref[0, :, 0:HD]
        values = kv_ref[0, :, HD:2 * HD]
        q = jnp.concatenate([q_ref[0, :, h * HD:(h + 1) * HD] for h in range(heads)], axis=0)
        s = lax.dot_general(
            q, keys, (((1,), (1,)), ((), ())), preferred_element_type=jnp.float32
        ) * (1.0 / math.sqrt(HD))
        old = peak_sc[j]
        new = jnp.maximum(old, jnp.max(s, axis=1, keepdims=True))
        fade = jnp.exp(old - new)
        p = jnp.exp(s - new)
        total_sc[j] = fade * total_sc[j] + jnp.sum(p, axis=1, keepdims=True)
        acc_sc[j] = fade * acc_sc[j] + jnp.dot(
            p.astype(jnp.bfloat16), values, preferred_element_type=jnp.float32
        )
        peak_sc[j] = new

    @pl.when(k == cap - 1)
    def _():
        acc_out[0] = acc_sc[...].astype(acc_out.dtype)
        eye = lax.broadcasted_iota(jnp.int32, (QLEN, QLEN), 0) == lax.broadcasted_iota(
            jnp.int32, (QLEN, QLEN), 1
        )
        for j in range(peak_sc.shape[0]):
            for h in range(heads):
                rows = pl.ds(h * QLEN, QLEN)
                peak_out[0, j, pl.ds(h, 1), :] = jnp.sum(
                    jnp.where(eye, peak_sc[j, rows, :], 0.0), axis=0, keepdims=True
                )
                total_out[0, j, pl.ds(h, 1), :] = jnp.sum(
                    jnp.where(eye, total_sc[j, rows, :], 0.0), axis=0, keepdims=True
                )


def slot_attention(rows, pick, valid, which, q_blocks, store, n_req, cap, n_query):
    width = q_blocks.shape[2]
    heads = width // HD
    n_slots = n_req * cap
    stacked = heads * QLEN
    flops = n_slots * heads * QLEN * PLEN * HD * 4
    return pl.pallas_call(
        slot_kernel,
        out_shape=(
            jax.ShapeDtypeStruct((n_req, n_query, stacked, HD), jnp.bfloat16),
            jax.ShapeDtypeStruct((n_req, n_query, heads, QLEN), jnp.float32),
            jax.ShapeDtypeStruct((n_req, n_query, heads, QLEN), jnp.float32),
        ),
        grid_spec=pltpu.PrefetchScalarGridSpec(
            num_scalar_prefetch=4,
            grid=(n_req, cap),
            in_specs=[
                pl.BlockSpec((1, QLEN, width), lambda r, k, rw, pk, vd, wh: (pk[r * cap + k], 0, 0)),
                pl.BlockSpec((1, PLEN, 2 * HD), lambda r, k, rw, pk, vd, wh: (rw[r * cap + k], 0, 0)),
            ],
            out_specs=[
                pl.BlockSpec((1, n_query, stacked, HD), lambda r, k, rw, pk, vd, wh: (r, 0, 0, 0)),
                pl.BlockSpec((1, n_query, heads, QLEN), lambda r, k, rw, pk, vd, wh: (r, 0, 0, 0)),
                pl.BlockSpec((1, n_query, heads, QLEN), lambda r, k, rw, pk, vd, wh: (r, 0, 0, 0)),
            ],
            scratch_shapes=[
                pltpu.VMEM((n_query, stacked, HD), jnp.float32),
                pltpu.VMEM((n_query, stacked, 1), jnp.float32),
                pltpu.VMEM((n_query, stacked, 1), jnp.float32),
            ],
        ),
        cost_estimate=pl.CostEstimate(
            flops=flops,
            transcendentals=n_slots * heads * QLEN * PLEN,
            bytes_accessed=n_slots * (QLEN * width * 2 + PLEN * 2 * HD * 2)
            + n_req * n_query * stacked * HD * 2,
        ),
    )(rows, pick, valid, which, q_blocks, store)


def own_part(query_rows, own_rows):
    count, tokens, width = query_rows.shape
    heads = width // HD
    q = query_rows.reshape(count, tokens, heads, HD)
    keys = own_rows[:, :, 0:HD]
    values = own_rows[:, :, HD:2 * HD]
    s = jnp.einsum("qthd,qld->qhtl", q, keys, preferred_element_type=jnp.float32) / math.sqrt(HD)
    visible = jnp.arange(tokens)[None, :] <= jnp.arange(tokens)[:, None]
    s = jnp.where(visible, s, -jnp.inf)
    m = jnp.max(s, axis=-1, keepdims=True)
    p = jnp.exp(s - m)
    total = jnp.sum(p, axis=-1, keepdims=True)
    acc = jnp.einsum(
        "qhtl,qld->qhtd", p.astype(jnp.bfloat16), values, preferred_element_type=jnp.float32
    )
    return acc, m, total


def shards(queries, own_kv, passage_store, out_weight, passage_slot, retrieved):
    n_cache = lax.axis_size("cache")
    store_count = passage_store.shape[0]
    slot_total = passage_slot.shape[0]
    query_count, per_query = retrieved.shape
    width = queries.shape[1]
    heads = width // HD
    wanted_count = query_count * per_query
    capacity = max(2, (2 * wanted_count + n_cache - 1) // n_cache)
    wanted = retrieved.reshape(wanted_count)
    id_match = wanted[:, None] == jnp.arange(slot_total, dtype=jnp.int32)[None, :]
    store_slots = jnp.sum(jnp.where(id_match, passage_slot[None, :], 0), axis=1)
    owners = store_slots // store_count
    local_rows = store_slots % store_count
    places = jnp.arange(wanted_count, dtype=jnp.int32)
    earlier = (owners[None, :] == owners[:, None]) & (places[None, :] < places[:, None])
    order_rank = jnp.sum(earlier, axis=1)
    flat_slot = owners * capacity + order_rank
    slot_match = flat_slot[:, None] == jnp.arange(n_cache * capacity, dtype=jnp.int32)[None, :]
    send_rows = jnp.sum(jnp.where(slot_match, local_rows[:, None], 0), axis=0)
    send_query = jnp.sum(jnp.where(slot_match, (places // per_query)[:, None], 0), axis=0)
    send_valid = jnp.sum(slot_match.astype(jnp.int32), axis=0)
    info = jnp.stack([send_rows, send_query, send_valid], axis=0).reshape(3, n_cache, capacity)
    asked = lax.all_to_all(info, "cache", split_axis=1, concat_axis=1, tiled=True)
    asked_rows = asked[0].reshape(n_cache * capacity)
    asked_query = asked[1]
    requester = jnp.arange(n_cache, dtype=jnp.int32)[:, None]
    pick = (requester * query_count + asked_query).reshape(n_cache * capacity)

    everyone_q = lax.all_gather(queries, "cache", axis=0, tiled=True)
    q_blocks = everyone_q.reshape(n_cache * query_count, QLEN, width)
    merged_acc, merged_peak, merged_total = slot_attention(
        asked_rows, pick, asked[2].reshape(n_cache * capacity), asked_query.reshape(n_cache * capacity),
        q_blocks, passage_store, n_cache, capacity, query_count,
    )
    merged_acc = merged_acc.reshape(n_cache, query_count, heads, QLEN, HD)
    stats = jnp.stack([merged_peak, merged_total], axis=2)
    back_acc = lax.all_to_all(
        merged_acc, "cache", split_axis=0, concat_axis=0, tiled=True
    )
    back_stats = lax.all_to_all(stats, "cache", split_axis=0, concat_axis=0, tiled=True)

    own_acc, own_peak, own_total = own_part(
        queries.reshape(query_count, QLEN, width),
        own_kv.reshape(query_count, QLEN, own_kv.shape[1]),
    )
    far_peak = back_stats[:, :, 0][..., None]
    far_total = back_stats[:, :, 1][..., None]
    top = jnp.maximum(jnp.max(far_peak, axis=0), own_peak)
    far_scale = jnp.exp(far_peak - top[None])
    own_scale = jnp.exp(own_peak - top)
    numer = jnp.sum(far_scale * back_acc.astype(jnp.float32), axis=0) + own_scale * own_acc
    denom = jnp.sum(far_scale * far_total, axis=0) + own_scale * own_total
    attended = (numer / denom).astype(jnp.bfloat16)
    attended = jnp.transpose(attended, (0, 2, 1, 3)).reshape(query_count * QLEN, width)
    return project(attended, out_weight)


def project(attended, out_weight):
    n_cache = lax.axis_size("cache")
    n_stream = lax.axis_size("stream")
    rows = attended.shape[0]
    group = n_cache // n_stream
    everyone = lax.all_gather(attended, "cache", axis=0, tiled=True)
    partial_sums = jnp.dot(everyone, out_weight, preferred_element_type=jnp.float32)
    reduced = lax.psum_scatter(
        partial_sums.astype(jnp.bfloat16), "stream", scatter_dimension=0, tiled=True
    )
    me = lax.axis_index("cache")
    width = reduced.shape[1]
    out = jnp.zeros((rows, group * width), reduced.dtype)
    for r in range(group):
        take = (me % group + r) % group
        piece = lax.dynamic_slice_in_dim(reduced, take * rows, rows, axis=0)
        perm = []
        for c in range(n_cache):
            for s in range(n_stream):
                dst_c = s * group + (c % group + r) % group
                dst_s = c // group
                perm.append((c * n_stream + s, dst_c * n_stream + dst_s))
        got = lax.ppermute(piece, ("cache", "stream"), perm)
        put = (me - r) % group
        out = lax.dynamic_update_slice_in_dim(out, got, put * width, axis=1)
    return out


def solution(mesh):
    return jax.shard_map(
        shards,
        mesh=mesh,
        in_specs=(
            P("cache", "stream"),
            P("cache", "stream"),
            P("cache", None, "stream"),
            P("stream", "cache"),
            P(),
            P("cache", None),
        ),
        out_specs=P("cache", "stream"),
        check_vma=False,
    )
```

```python
import math

import jax
import jax.numpy as jnp
from jax import lax
from jax.experimental import pallas as pl
from jax.experimental.pallas import tpu as pltpu
from jax.sharding import PartitionSpec as P

HD = 128
QLEN = 128
PLEN = 512
FLOOR = -1e30


def slot_kernel(rows_ref, pick_ref, valid_ref, which_ref, q_ref, kv_ref,
                acc_out, peak_out, total_out, acc_sc, peak_sc, total_sc):
    r = pl.program_id(0)
    k = pl.program_id(1)
    cap = pl.num_programs(1)
    heads = q_ref.shape[2] // HD

    @pl.when(k == 0)
    def _():
        acc_sc[...] = jnp.zeros_like(acc_sc)
        peak_sc[...] = jnp.full_like(peak_sc, FLOOR)
        total_sc[...] = jnp.zeros_like(total_sc)

    i = r * cap + k

    @pl.when(valid_ref[i] > 0)
    def _():
        j = which_ref[i]
        keys = kv_ref[0, :, 0:HD]
        values = kv_ref[0, :, HD:2 * HD]
        q = jnp.concatenate([q_ref[0, :, h * HD:(h + 1) * HD] for h in range(heads)], axis=0)
        s = lax.dot_general(
            q, keys, (((1,), (1,)), ((), ())), preferred_element_type=jnp.float32
        ) * (1.0 / math.sqrt(HD))
        old = peak_sc[j]
        new = jnp.maximum(old, jnp.max(s, axis=1, keepdims=True))
        fade = jnp.exp(old - new)
        p = jnp.exp(s - new)
        total_sc[j] = fade * total_sc[j] + jnp.sum(p, axis=1, keepdims=True)
        acc_sc[j] = fade * acc_sc[j] + jnp.dot(
            p.astype(jnp.bfloat16), values, preferred_element_type=jnp.float32
        )
        peak_sc[j] = new

    @pl.when(k == cap - 1)
    def _():
        acc_out[0] = acc_sc[...].astype(acc_out.dtype)
        eye = lax.broadcasted_iota(jnp.int32, (QLEN, QLEN), 0) == lax.broadcasted_iota(
            jnp.int32, (QLEN, QLEN), 1
        )
        for j in range(peak_sc.shape[0]):
            for h in range(heads):
                rows = pl.ds(h * QLEN, QLEN)
                peak_out[0, j, pl.ds(h, 1), :] = jnp.sum(
                    jnp.where(eye, peak_sc[j, rows, :], 0.0), axis=0, keepdims=True
                )
                total_out[0, j, pl.ds(h, 1), :] = jnp.sum(
                    jnp.where(eye, total_sc[j, rows, :], 0.0), axis=0, keepdims=True
                )


def slot_attention(rows, pick, valid, which, q_blocks, store, n_req, cap, n_query):
    width = q_blocks.shape[2]
    heads = width // HD
    n_slots = n_req * cap
    stacked = heads * QLEN
    flops = n_slots * heads * QLEN * PLEN * HD * 4
    return pl.pallas_call(
        slot_kernel,
        out_shape=(
            jax.ShapeDtypeStruct((n_req, n_query, stacked, HD), jnp.bfloat16),
            jax.ShapeDtypeStruct((n_req, n_query, heads, QLEN), jnp.float32),
            jax.ShapeDtypeStruct((n_req, n_query, heads, QLEN), jnp.float32),
        ),
        grid_spec=pltpu.PrefetchScalarGridSpec(
            num_scalar_prefetch=4,
            grid=(n_req, cap),
            in_specs=[
                pl.BlockSpec((1, QLEN, width), lambda r, k, rw, pk, vd, wh: (pk[r * cap + k], 0, 0)),
                pl.BlockSpec((1, PLEN, 2 * HD), lambda r, k, rw, pk, vd, wh: (rw[r * cap + k], 0, 0)),
            ],
            out_specs=[
                pl.BlockSpec((1, n_query, stacked, HD), lambda r, k, rw, pk, vd, wh: (r, 0, 0, 0)),
                pl.BlockSpec((1, n_query, heads, QLEN), lambda r, k, rw, pk, vd, wh: (r, 0, 0, 0)),
                pl.BlockSpec((1, n_query, heads, QLEN), lambda r, k, rw, pk, vd, wh: (r, 0, 0, 0)),
            ],
            scratch_shapes=[
                pltpu.VMEM((n_query, stacked, HD), jnp.float32),
                pltpu.VMEM((n_query, stacked, 1), jnp.float32),
                pltpu.VMEM((n_query, stacked, 1), jnp.float32),
            ],
        ),
        cost_estimate=pl.CostEstimate(
            flops=flops,
            transcendentals=n_slots * heads * QLEN * PLEN,
            bytes_accessed=n_slots * (QLEN * width * 2 + PLEN * 2 * HD * 2)
            + n_req * n_query * stacked * HD * 2,
        ),
    )(rows, pick, valid, which, q_blocks, store)


def own_part(query_rows, own_rows):
    count, tokens, width = query_rows.shape
    heads = width // HD
    q = query_rows.reshape(count, tokens, heads, HD)
    keys = own_rows[:, :, 0:HD]
    values = own_rows[:, :, HD:2 * HD]
    s = jnp.einsum("qthd,qld->qhtl", q, keys, preferred_element_type=jnp.float32) / math.sqrt(HD)
    visible = jnp.arange(tokens)[None, :] <= jnp.arange(tokens)[:, None]
    s = jnp.where(visible, s, -jnp.inf)
    m = jnp.max(s, axis=-1, keepdims=True)
    p = jnp.exp(s - m)
    total = jnp.sum(p, axis=-1, keepdims=True)
    acc = jnp.einsum(
        "qhtl,qld->qhtd", p.astype(jnp.bfloat16), values, preferred_element_type=jnp.float32
    )
    return acc, m, total


def shards(queries, own_kv, passage_store, out_weight, passage_slot, retrieved):
    n_cache = lax.axis_size("cache")
    store_count = passage_store.shape[0]
    slot_total = passage_slot.shape[0]
    query_count, per_query = retrieved.shape
    width = queries.shape[1]
    heads = width // HD
    wanted_count = query_count * per_query
    capacity = max(2, (2 * wanted_count + n_cache - 1) // n_cache)
    wanted = retrieved.reshape(wanted_count)
    id_match = wanted[:, None] == jnp.arange(slot_total, dtype=jnp.int32)[None, :]
    store_slots = jnp.sum(jnp.where(id_match, passage_slot[None, :], 0), axis=1)
    owners = store_slots // store_count
    local_rows = store_slots % store_count
    places = jnp.arange(wanted_count, dtype=jnp.int32)
    earlier = (owners[None, :] == owners[:, None]) & (places[None, :] < places[:, None])
    order_rank = jnp.sum(earlier, axis=1)
    flat_slot = owners * capacity + order_rank
    slot_match = flat_slot[:, None] == jnp.arange(n_cache * capacity, dtype=jnp.int32)[None, :]
    send_rows = jnp.sum(jnp.where(slot_match, local_rows[:, None], 0), axis=0)
    send_query = jnp.sum(jnp.where(slot_match, (places // per_query)[:, None], 0), axis=0)
    send_valid = jnp.sum(slot_match.astype(jnp.int32), axis=0)
    info = jnp.stack([send_rows, send_query, send_valid], axis=0).reshape(3, n_cache, capacity)
    asked = lax.all_to_all(info, "cache", split_axis=1, concat_axis=1, tiled=True)
    asked_rows = asked[0].reshape(n_cache * capacity)
    asked_query = asked[1]
    me = lax.axis_index("cache")
    q_local = queries.reshape(query_count, QLEN, width)
    far_acc = []
    far_stats = []
    for off in range(n_cache):
        source = (me + n_cache - off) % n_cache
        if off == 0:
            q_here = q_local
        else:
            q_here = lax.ppermute(
                q_local, "cache", [(c, (c + off) % n_cache) for c in range(n_cache)]
            )
        mine = lax.dynamic_index_in_dim(asked, source, axis=1, keepdims=False)
        acc_r, peak_r, total_r = slot_attention(
            mine[0], mine[1], mine[2], mine[1], q_here, passage_store, 1, capacity, query_count,
        )
        acc_r = acc_r.reshape(query_count, heads, QLEN, HD)
        stats_r = jnp.stack([peak_r[0], total_r[0]], axis=1)
        if off != 0:
            home = [(c, (c + n_cache - off) % n_cache) for c in range(n_cache)]
            acc_r = lax.ppermute(acc_r, "cache", home)
            stats_r = lax.ppermute(stats_r, "cache", home)
        far_acc.append(acc_r)
        far_stats.append(stats_r)
    back_acc = jnp.stack(far_acc, axis=0)
    back_stats = jnp.stack(far_stats, axis=0)

    own_acc, own_peak, own_total = own_part(
        queries.reshape(query_count, QLEN, width),
        own_kv.reshape(query_count, QLEN, own_kv.shape[1]),
    )
    far_peak = back_stats[:, :, 0][..., None]
    far_total = back_stats[:, :, 1][..., None]
    top = jnp.maximum(jnp.max(far_peak, axis=0), own_peak)
    far_scale = jnp.exp(far_peak - top[None])
    own_scale = jnp.exp(own_peak - top)
    numer = jnp.sum(far_scale * back_acc.astype(jnp.float32), axis=0) + own_scale * own_acc
    denom = jnp.sum(far_scale * far_total, axis=0) + own_scale * own_total
    attended = (numer / denom).astype(jnp.bfloat16)
    attended = jnp.transpose(attended, (0, 2, 1, 3)).reshape(query_count * QLEN, width)
    return project(attended, out_weight)


def project(attended, out_weight):
    n_cache = lax.axis_size("cache")
    n_stream = lax.axis_size("stream")
    rows = attended.shape[0]
    group = n_cache // n_stream
    everyone = lax.all_gather(attended, "cache", axis=0, tiled=True)
    partial_sums = jnp.dot(everyone, out_weight, preferred_element_type=jnp.float32)
    reduced = lax.psum_scatter(
        partial_sums.astype(jnp.bfloat16), "stream", scatter_dimension=0, tiled=True
    )
    me = lax.axis_index("cache")
    width = reduced.shape[1]
    out = jnp.zeros((rows, group * width), reduced.dtype)
    for r in range(group):
        take = (me % group + r) % group
        piece = lax.dynamic_slice_in_dim(reduced, take * rows, rows, axis=0)
        perm = []
        for c in range(n_cache):
            for s in range(n_stream):
                dst_c = s * group + (c % group + r) % group
                dst_s = c // group
                perm.append((c * n_stream + s, dst_c * n_stream + dst_s))
        got = lax.ppermute(piece, ("cache", "stream"), perm)
        put = (me - r) % group
        out = lax.dynamic_update_slice_in_dim(out, got, put * width, axis=1)
    return out


def solution(mesh):
    return jax.shard_map(
        shards,
        mesh=mesh,
        in_specs=(
            P("cache", "stream"),
            P("cache", "stream"),
            P("cache", None, "stream"),
            P("stream", "cache"),
            P(),
            P("cache", None),
        ),
        out_specs=P("cache", "stream"),
        check_vma=False,
    )
```

```python
import functools
import math

import jax
import jax.numpy as jnp
from jax import lax
from jax.experimental import pallas as pl
from jax.experimental.pallas import tpu as pltpu
from jax.sharding import PartitionSpec as P

HD = 128
QLEN = 128
PLEN = 512
FLOOR = -1e30


def slot_kernel(only, rows_ref, pick_ref, valid_ref, which_ref, q_ref, kv_ref,
                acc_out, peak_out, total_out, acc_sc, peak_sc, total_sc):
    r = pl.program_id(0)
    k = pl.program_id(1)
    cap = pl.num_programs(1)
    heads = q_ref.shape[2] // HD

    @pl.when(k == 0)
    def _():
        acc_sc[...] = jnp.zeros_like(acc_sc)
        peak_sc[...] = jnp.full_like(peak_sc, FLOOR)
        total_sc[...] = jnp.zeros_like(total_sc)

    i = r * cap + k

    @pl.when((valid_ref[i] > 0) & (which_ref[i] == only))
    def _():
        j = 0
        keys = kv_ref[0, :, 0:HD]
        values = kv_ref[0, :, HD:2 * HD]
        q = jnp.concatenate([q_ref[0, :, h * HD:(h + 1) * HD] for h in range(heads)], axis=0)
        s = lax.dot_general(
            q, keys, (((1,), (1,)), ((), ())), preferred_element_type=jnp.float32
        ) * (1.0 / math.sqrt(HD))
        old = peak_sc[j]
        new = jnp.maximum(old, jnp.max(s, axis=1, keepdims=True))
        fade = jnp.exp(old - new)
        p = jnp.exp(s - new)
        total_sc[j] = fade * total_sc[j] + jnp.sum(p, axis=1, keepdims=True)
        acc_sc[j] = fade * acc_sc[j] + jnp.dot(
            p.astype(jnp.bfloat16), values, preferred_element_type=jnp.float32
        )
        peak_sc[j] = new

    @pl.when(k == cap - 1)
    def _():
        acc_out[0] = acc_sc[...].astype(acc_out.dtype)
        eye = lax.broadcasted_iota(jnp.int32, (QLEN, QLEN), 0) == lax.broadcasted_iota(
            jnp.int32, (QLEN, QLEN), 1
        )
        for j in range(peak_sc.shape[0]):
            for h in range(heads):
                rows = pl.ds(h * QLEN, QLEN)
                peak_out[0, j, pl.ds(h, 1), :] = jnp.sum(
                    jnp.where(eye, peak_sc[j, rows, :], 0.0), axis=0, keepdims=True
                )
                total_out[0, j, pl.ds(h, 1), :] = jnp.sum(
                    jnp.where(eye, total_sc[j, rows, :], 0.0), axis=0, keepdims=True
                )


def slot_attention(rows, pick, valid, which, q_blocks, store, n_req, cap, only):
    n_query = 1
    width = q_blocks.shape[2]
    heads = width // HD
    n_slots = n_req * cap
    stacked = heads * QLEN
    flops = n_slots * heads * QLEN * PLEN * HD * 4
    return pl.pallas_call(
        functools.partial(slot_kernel, only),
        out_shape=(
            jax.ShapeDtypeStruct((n_req, n_query, stacked, HD), jnp.bfloat16),
            jax.ShapeDtypeStruct((n_req, n_query, heads, QLEN), jnp.float32),
            jax.ShapeDtypeStruct((n_req, n_query, heads, QLEN), jnp.float32),
        ),
        grid_spec=pltpu.PrefetchScalarGridSpec(
            num_scalar_prefetch=4,
            grid=(n_req, cap),
            in_specs=[
                pl.BlockSpec((1, QLEN, width), lambda r, k, rw, pk, vd, wh: (pk[r * cap + k], 0, 0)),
                pl.BlockSpec((1, PLEN, 2 * HD), lambda r, k, rw, pk, vd, wh: (rw[r * cap + k], 0, 0)),
            ],
            out_specs=[
                pl.BlockSpec((1, n_query, stacked, HD), lambda r, k, rw, pk, vd, wh: (r, 0, 0, 0)),
                pl.BlockSpec((1, n_query, heads, QLEN), lambda r, k, rw, pk, vd, wh: (r, 0, 0, 0)),
                pl.BlockSpec((1, n_query, heads, QLEN), lambda r, k, rw, pk, vd, wh: (r, 0, 0, 0)),
            ],
            scratch_shapes=[
                pltpu.VMEM((n_query, stacked, HD), jnp.float32),
                pltpu.VMEM((n_query, stacked, 1), jnp.float32),
                pltpu.VMEM((n_query, stacked, 1), jnp.float32),
            ],
        ),
        cost_estimate=pl.CostEstimate(
            flops=flops // 2,
            transcendentals=n_slots * heads * QLEN * PLEN // 2,
            bytes_accessed=n_slots * (QLEN * width * 2 + PLEN * 2 * HD * 2)
            + n_req * n_query * stacked * HD * 2,
        ),
    )(rows, pick, valid, which, q_blocks, store)


def own_part(query_rows, own_rows):
    count, tokens, width = query_rows.shape
    heads = width // HD
    q = query_rows.reshape(count, tokens, heads, HD)
    keys = own_rows[:, :, 0:HD]
    values = own_rows[:, :, HD:2 * HD]
    s = jnp.einsum("qthd,qld->qhtl", q, keys, preferred_element_type=jnp.float32) / math.sqrt(HD)
    visible = jnp.arange(tokens)[None, :] <= jnp.arange(tokens)[:, None]
    s = jnp.where(visible, s, -jnp.inf)
    m = jnp.max(s, axis=-1, keepdims=True)
    p = jnp.exp(s - m)
    total = jnp.sum(p, axis=-1, keepdims=True)
    acc = jnp.einsum(
        "qhtl,qld->qhtd", p.astype(jnp.bfloat16), values, preferred_element_type=jnp.float32
    )
    return acc, m, total


def shards(queries, own_kv, passage_store, out_weight, passage_slot, retrieved):
    n_cache = lax.axis_size("cache")
    store_count = passage_store.shape[0]
    slot_total = passage_slot.shape[0]
    query_count, per_query = retrieved.shape
    width = queries.shape[1]
    heads = width // HD
    wanted_count = query_count * per_query
    capacity = max(2, (2 * wanted_count + n_cache - 1) // n_cache)
    wanted = retrieved.reshape(wanted_count)
    id_match = wanted[:, None] == jnp.arange(slot_total, dtype=jnp.int32)[None, :]
    store_slots = jnp.sum(jnp.where(id_match, passage_slot[None, :], 0), axis=1)
    owners = store_slots // store_count
    local_rows = store_slots % store_count
    places = jnp.arange(wanted_count, dtype=jnp.int32)
    earlier = (owners[None, :] == owners[:, None]) & (places[None, :] < places[:, None])
    order_rank = jnp.sum(earlier, axis=1)
    flat_slot = owners * capacity + order_rank
    slot_match = flat_slot[:, None] == jnp.arange(n_cache * capacity, dtype=jnp.int32)[None, :]
    send_rows = jnp.sum(jnp.where(slot_match, local_rows[:, None], 0), axis=0)
    send_query = jnp.sum(jnp.where(slot_match, (places // per_query)[:, None], 0), axis=0)
    send_valid = jnp.sum(slot_match.astype(jnp.int32), axis=0)
    info = jnp.stack([send_rows, send_query, send_valid], axis=0).reshape(3, n_cache, capacity)
    asked = lax.all_to_all(info, "cache", split_axis=1, concat_axis=1, tiled=True)
    asked_rows = asked[0].reshape(n_cache * capacity)
    asked_query = asked[1]
    requester = jnp.arange(n_cache, dtype=jnp.int32)[:, None]
    pick = (requester * query_count + asked_query).reshape(n_cache * capacity)

    everyone_q = lax.all_gather(queries, "cache", axis=0, tiled=True)
    q_blocks = everyone_q.reshape(n_cache * query_count, QLEN, width)
    own_acc, own_peak, own_total = own_part(
        queries.reshape(query_count, QLEN, width),
        own_kv.reshape(query_count, QLEN, own_kv.shape[1]),
    )
    outs = []
    for only in range(query_count):
        merged_acc, merged_peak, merged_total = slot_attention(
            asked_rows, pick, asked[2].reshape(n_cache * capacity), asked_query.reshape(n_cache * capacity),
            q_blocks, passage_store, n_cache, capacity, only,
        )
        merged_acc = merged_acc.reshape(n_cache, heads, QLEN, HD)
        stats = jnp.stack([merged_peak[:, 0], merged_total[:, 0]], axis=1)
        back_acc = lax.all_to_all(merged_acc, "cache", split_axis=0, concat_axis=0, tiled=True)
        back_stats = lax.all_to_all(stats, "cache", split_axis=0, concat_axis=0, tiled=True)
        far_peak = back_stats[:, 0][..., None]
        far_total = back_stats[:, 1][..., None]
        top = jnp.maximum(jnp.max(far_peak, axis=0), own_peak[only])
        far_scale = jnp.exp(far_peak - top[None])
        own_scale = jnp.exp(own_peak[only] - top)
        numer = jnp.sum(far_scale * back_acc.astype(jnp.float32), axis=0) + own_scale * own_acc[only]
        denom = jnp.sum(far_scale * far_total, axis=0) + own_scale * own_total[only]
        attended = (numer / denom).astype(jnp.bfloat16)
        attended = jnp.transpose(attended, (1, 0, 2)).reshape(QLEN, width)
        outs.append(project(attended, out_weight))
    return jnp.concatenate(outs, axis=0)


def project(attended, out_weight):
    n_cache = lax.axis_size("cache")
    n_stream = lax.axis_size("stream")
    rows = attended.shape[0]
    group = n_cache // n_stream
    everyone = lax.all_gather(attended, "cache", axis=0, tiled=True)
    partial_sums = jnp.dot(everyone, out_weight, preferred_element_type=jnp.float32)
    reduced = lax.psum_scatter(
        partial_sums.astype(jnp.bfloat16), "stream", scatter_dimension=0, tiled=True
    )
    me = lax.axis_index("cache")
    width = reduced.shape[1]
    out = jnp.zeros((rows, group * width), reduced.dtype)
    for r in range(group):
        take = (me % group + r) % group
        piece = lax.dynamic_slice_in_dim(reduced, take * rows, rows, axis=0)
        perm = []
        for c in range(n_cache):
            for s in range(n_stream):
                dst_c = s * group + (c % group + r) % group
                dst_s = c // group
                perm.append((c * n_stream + s, dst_c * n_stream + dst_s))
        got = lax.ppermute(piece, ("cache", "stream"), perm)
        put = (me - r) % group
        out = lax.dynamic_update_slice_in_dim(out, got, put * width, axis=1)
    return out


def solution(mesh):
    return jax.shard_map(
        shards,
        mesh=mesh,
        in_specs=(
            P("cache", "stream"),
            P("cache", "stream"),
            P("cache", None, "stream"),
            P("stream", "cache"),
            P(),
            P("cache", None),
        ),
        out_specs=P("cache", "stream"),
        check_vma=False,
    )
```

```python
import math

import jax
import jax.numpy as jnp
from jax import lax
from jax.experimental import pallas as pl
from jax.experimental.pallas import tpu as pltpu
from jax.sharding import PartitionSpec as P

HD = 128
QLEN = 128
PLEN = 512
FLOOR = -1e30


def slot_kernel(rows_ref, pick_ref, valid_ref, which_ref, q0_ref, kv0_ref, q1_ref, kv1_ref,
                acc_out, peak_out, total_out, acc_sc, peak_sc, total_sc):
    r = pl.program_id(0)
    k = pl.program_id(1)
    pairs = pl.num_programs(1)
    heads = q0_ref.shape[2] // HD
    fold = math.log2(math.e) / math.sqrt(HD)

    @pl.when(k == 0)
    def _():
        acc_sc[...] = jnp.zeros_like(acc_sc)
        peak_sc[...] = jnp.full_like(peak_sc, FLOOR)
        total_sc[...] = jnp.zeros_like(total_sc)

    for half, q_ref, kv_ref in ((0, q0_ref, kv0_ref), (1, q1_ref, kv1_ref)):
        i = (r * pairs + k) * 2 + half

        @pl.when(valid_ref[i] > 0)
        def _():
            j = which_ref[i]
            keys = kv_ref[0, :, 0:HD]
            values = kv_ref[0, :, HD:2 * HD]
            q = jnp.concatenate([q_ref[0, :, h * HD:(h + 1) * HD] for h in range(heads)], axis=0)
            s = lax.dot_general(
                q, keys, (((1,), (1,)), ((), ())), preferred_element_type=jnp.float32
            )
            old = peak_sc[j]
            new = jnp.maximum(old, jnp.max(s, axis=1, keepdims=True))
            fade = jnp.exp2((old - new) * fold)
            p = jnp.exp2((s - new) * fold)
            total_sc[j] = fade * total_sc[j] + jnp.sum(p, axis=1, keepdims=True)
            acc_sc[j] = fade * acc_sc[j] + jnp.dot(
                p.astype(jnp.bfloat16), values, preferred_element_type=jnp.float32
            )
            peak_sc[j] = new

    @pl.when(k == pairs - 1)
    def _():
        acc_out[0] = acc_sc[...].astype(acc_out.dtype)
        eye = lax.broadcasted_iota(jnp.int32, (QLEN, QLEN), 0) == lax.broadcasted_iota(
            jnp.int32, (QLEN, QLEN), 1
        )
        for j in range(peak_sc.shape[0]):
            for h in range(heads):
                rows = pl.ds(h * QLEN, QLEN)
                peak_out[0, j, pl.ds(h, 1), :] = jnp.sum(
                    jnp.where(eye, peak_sc[j, rows, :], 0.0), axis=0, keepdims=True
                ) * (1.0 / math.sqrt(HD))
                total_out[0, j, pl.ds(h, 1), :] = jnp.sum(
                    jnp.where(eye, total_sc[j, rows, :], 0.0), axis=0, keepdims=True
                )


def slot_attention(rows, pick, valid, which, q_blocks, store, n_req, cap, n_query):
    width = q_blocks.shape[2]
    heads = width // HD
    n_slots = n_req * cap
    pairs = cap // 2
    stacked = heads * QLEN
    flops = n_slots * heads * QLEN * PLEN * HD * 4
    q_spec = lambda half: pl.BlockSpec(
        (1, QLEN, width), lambda r, k, rw, pk, vd, wh: (pk[(r * pairs + k) * 2 + half], 0, 0)
    )
    kv_spec = lambda half: pl.BlockSpec(
        (1, PLEN, 2 * HD), lambda r, k, rw, pk, vd, wh: (rw[(r * pairs + k) * 2 + half], 0, 0)
    )
    return pl.pallas_call(
        slot_kernel,
        out_shape=(
            jax.ShapeDtypeStruct((n_req, n_query, stacked, HD), jnp.bfloat16),
            jax.ShapeDtypeStruct((n_req, n_query, heads, QLEN), jnp.float32),
            jax.ShapeDtypeStruct((n_req, n_query, heads, QLEN), jnp.float32),
        ),
        grid_spec=pltpu.PrefetchScalarGridSpec(
            num_scalar_prefetch=4,
            grid=(n_req, pairs),
            in_specs=[q_spec(0), kv_spec(0), q_spec(1), kv_spec(1)],
            out_specs=[
                pl.BlockSpec((1, n_query, stacked, HD), lambda r, k, rw, pk, vd, wh: (r, 0, 0, 0)),
                pl.BlockSpec((1, n_query, heads, QLEN), lambda r, k, rw, pk, vd, wh: (r, 0, 0, 0)),
                pl.BlockSpec((1, n_query, heads, QLEN), lambda r, k, rw, pk, vd, wh: (r, 0, 0, 0)),
            ],
            scratch_shapes=[
                pltpu.VMEM((n_query, stacked, HD), jnp.float32),
                pltpu.VMEM((n_query, stacked, 1), jnp.float32),
                pltpu.VMEM((n_query, stacked, 1), jnp.float32),
            ],
        ),
        cost_estimate=pl.CostEstimate(
            flops=flops,
            transcendentals=n_slots * heads * QLEN * PLEN,
            bytes_accessed=n_slots * (QLEN * width * 2 + PLEN * 2 * HD * 2)
            + n_req * n_query * stacked * HD * 2,
        ),
    )(rows, pick, valid, which, q_blocks, store, q_blocks, store)


def own_part(query_rows, own_rows):
    count, tokens, width = query_rows.shape
    heads = width // HD
    q = query_rows.reshape(count, tokens, heads, HD)
    keys = own_rows[:, :, 0:HD]
    values = own_rows[:, :, HD:2 * HD]
    s = jnp.einsum("qthd,qld->qhtl", q, keys, preferred_element_type=jnp.float32) / math.sqrt(HD)
    visible = jnp.arange(tokens)[None, :] <= jnp.arange(tokens)[:, None]
    s = jnp.where(visible, s, -jnp.inf)
    m = jnp.max(s, axis=-1, keepdims=True)
    p = jnp.exp(s - m)
    total = jnp.sum(p, axis=-1, keepdims=True)
    acc = jnp.einsum(
        "qhtl,qld->qhtd", p.astype(jnp.bfloat16), values, preferred_element_type=jnp.float32
    )
    return acc, m, total


def shards(queries, own_kv, passage_store, out_weight, passage_slot, retrieved):
    n_cache = lax.axis_size("cache")
    store_count = passage_store.shape[0]
    slot_total = passage_slot.shape[0]
    query_count, per_query = retrieved.shape
    width = queries.shape[1]
    heads = width // HD
    wanted_count = query_count * per_query
    capacity = max(2, (2 * wanted_count + n_cache - 1) // n_cache)
    capacity += capacity % 2
    wanted = retrieved.reshape(wanted_count)
    id_match = wanted[:, None] == jnp.arange(slot_total, dtype=jnp.int32)[None, :]
    store_slots = jnp.sum(jnp.where(id_match, passage_slot[None, :], 0), axis=1)
    owners = store_slots // store_count
    local_rows = store_slots % store_count
    places = jnp.arange(wanted_count, dtype=jnp.int32)
    earlier = (owners[None, :] == owners[:, None]) & (places[None, :] < places[:, None])
    order_rank = jnp.sum(earlier, axis=1)
    flat_slot = owners * capacity + order_rank
    slot_match = flat_slot[:, None] == jnp.arange(n_cache * capacity, dtype=jnp.int32)[None, :]
    send_rows = jnp.sum(jnp.where(slot_match, local_rows[:, None], 0), axis=0)
    send_query = jnp.sum(jnp.where(slot_match, (places // per_query)[:, None], 0), axis=0)
    send_valid = jnp.sum(slot_match.astype(jnp.int32), axis=0)
    info = jnp.stack([send_rows, send_query, send_valid], axis=0).reshape(3, n_cache, capacity)
    asked = lax.all_to_all(info, "cache", split_axis=1, concat_axis=1, tiled=True)
    asked_rows = asked[0].reshape(n_cache * capacity)
    asked_query = asked[1]
    requester = jnp.arange(n_cache, dtype=jnp.int32)[:, None]
    pick = (requester * query_count + asked_query).reshape(n_cache * capacity)

    everyone_q = lax.all_gather(queries, "cache", axis=0, tiled=True)
    q_blocks = everyone_q.reshape(n_cache * query_count, QLEN, width)
    merged_acc, merged_peak, merged_total = slot_attention(
        asked_rows, pick, asked[2].reshape(n_cache * capacity), asked_query.reshape(n_cache * capacity),
        q_blocks, passage_store, n_cache, capacity, query_count,
    )
    merged_acc = merged_acc.reshape(n_cache, query_count, heads, QLEN, HD)
    stats = jnp.stack([merged_peak, merged_total], axis=2)
    back_acc = lax.all_to_all(
        merged_acc, "cache", split_axis=0, concat_axis=0, tiled=True
    )
    back_stats = lax.all_to_all(stats, "cache", split_axis=0, concat_axis=0, tiled=True)

    own_acc, own_peak, own_total = own_part(
        queries.reshape(query_count, QLEN, width),
        own_kv.reshape(query_count, QLEN, own_kv.shape[1]),
    )
    far_peak = back_stats[:, :, 0][..., None]
    far_total = back_stats[:, :, 1][..., None]
    top = jnp.maximum(jnp.max(far_peak, axis=0), own_peak)
    far_scale = jnp.exp(far_peak - top[None])
    own_scale = jnp.exp(own_peak - top)
    numer = jnp.sum(far_scale * back_acc.astype(jnp.float32), axis=0) + own_scale * own_acc
    denom = jnp.sum(far_scale * far_total, axis=0) + own_scale * own_total
    attended = (numer / denom).astype(jnp.bfloat16)
    attended = jnp.transpose(attended, (0, 2, 1, 3)).reshape(query_count * QLEN, width)
    return project(attended, out_weight)


def project(attended, out_weight):
    n_cache = lax.axis_size("cache")
    n_stream = lax.axis_size("stream")
    rows = attended.shape[0]
    group = n_cache // n_stream
    everyone = lax.all_gather(attended, "cache", axis=0, tiled=True)
    partial_sums = jnp.dot(everyone, out_weight, preferred_element_type=jnp.float32)
    reduced = lax.psum_scatter(
        partial_sums.astype(jnp.bfloat16), "stream", scatter_dimension=0, tiled=True
    )
    me = lax.axis_index("cache")
    width = reduced.shape[1]
    out = jnp.zeros((rows, group * width), reduced.dtype)
    for r in range(group):
        take = (me % group + r) % group
        piece = lax.dynamic_slice_in_dim(reduced, take * rows, rows, axis=0)
        perm = []
        for c in range(n_cache):
            for s in range(n_stream):
                dst_c = s * group + (c % group + r) % group
                dst_s = c // group
                perm.append((c * n_stream + s, dst_c * n_stream + dst_s))
        got = lax.ppermute(piece, ("cache", "stream"), perm)
        put = (me - r) % group
        out = lax.dynamic_update_slice_in_dim(out, got, put * width, axis=1)
    return out


def solution(mesh):
    return jax.shard_map(
        shards,
        mesh=mesh,
        in_specs=(
            P("cache", "stream"),
            P("cache", "stream"),
            P("cache", None, "stream"),
            P("stream", "cache"),
            P(),
            P("cache", None),
        ),
        out_specs=P("cache", "stream"),
        check_vma=False,
    )
```

```python
import math

import jax
import jax.numpy as jnp
from jax import lax
from jax.experimental import pallas as pl
from jax.experimental.pallas import tpu as pltpu
from jax.sharding import PartitionSpec as P

HD = 128
QLEN = 128
PLEN = 512
FLOOR = -1e30
LIVE = -1e20


def slot_kernel(rows_ref, pick_ref, valid_ref, which_ref, q0_ref, kv0_ref, q1_ref, kv1_ref,
                acc_out, peak_out, total_out, acc_sc, peak_sc, total_sc):
    r = pl.program_id(0)
    k = pl.program_id(1)
    pairs = pl.num_programs(1)
    heads = q0_ref.shape[2] // HD
    fold = math.log2(math.e) / math.sqrt(HD)

    @pl.when(k == 0)
    def _():
        acc_sc[...] = jnp.zeros_like(acc_sc)
        peak_sc[...] = jnp.full_like(peak_sc, FLOOR)
        total_sc[...] = jnp.zeros_like(total_sc)

    for half, q_ref, kv_ref in ((0, q0_ref, kv0_ref), (1, q1_ref, kv1_ref)):
        i = (r * pairs + k) * 2 + half

        @pl.when(valid_ref[i] > 0)
        def _():
            j = which_ref[i]
            keys = kv_ref[0, :, 0:HD]
            values = kv_ref[0, :, HD:2 * HD]
            q = jnp.concatenate([q_ref[0, :, h * HD:(h + 1) * HD] for h in range(heads)], axis=0)
            s = lax.dot_general(
                q, keys, (((1,), (1,)), ((), ())), preferred_element_type=jnp.float32
            )
            old = peak_sc[j]
            new = jnp.maximum(old, jnp.max(s, axis=1, keepdims=True))
            fade = jnp.exp2((old - new) * fold)
            p = jnp.exp2((s - new) * fold)
            total_sc[j] = fade * total_sc[j] + jnp.sum(p, axis=1, keepdims=True)
            acc_sc[j] = fade * acc_sc[j] + jnp.dot(
                p.astype(jnp.bfloat16), values, preferred_element_type=jnp.float32
            )
            peak_sc[j] = new

    @pl.when(k == pairs - 1)
    def _():
        acc_out[0] = acc_sc[...].astype(acc_out.dtype)
        eye = lax.broadcasted_iota(jnp.int32, (QLEN, QLEN), 0) == lax.broadcasted_iota(
            jnp.int32, (QLEN, QLEN), 1
        )
        for j in range(peak_sc.shape[0]):
            for h in range(heads):
                rows = pl.ds(h * QLEN, QLEN)
                peak_out[0, j, pl.ds(h, 1), :] = jnp.sum(
                    jnp.where(eye, peak_sc[j, rows, :], 0.0), axis=0, keepdims=True
                ) * (1.0 / math.sqrt(HD))
                total_out[0, j, pl.ds(h, 1), :] = jnp.sum(
                    jnp.where(eye, total_sc[j, rows, :], 0.0), axis=0, keepdims=True
                )


def slot_attention(rows, pick, valid, which, q_blocks, store, n_req, cap, n_query):
    width = q_blocks.shape[2]
    heads = width // HD
    n_slots = n_req * cap
    pairs = cap // 2
    stacked = heads * QLEN
    flops = n_slots * heads * QLEN * PLEN * HD * 4
    q_spec = lambda half: pl.BlockSpec(
        (1, QLEN, width), lambda r, k, rw, pk, vd, wh: (pk[(r * pairs + k) * 2 + half], 0, 0)
    )
    kv_spec = lambda half: pl.BlockSpec(
        (1, PLEN, 2 * HD), lambda r, k, rw, pk, vd, wh: (rw[(r * pairs + k) * 2 + half], 0, 0)
    )
    return pl.pallas_call(
        slot_kernel,
        out_shape=(
            jax.ShapeDtypeStruct((n_req, n_query, stacked, HD), jnp.float32),
            jax.ShapeDtypeStruct((n_req, n_query, heads, QLEN), jnp.float32),
            jax.ShapeDtypeStruct((n_req, n_query, heads, QLEN), jnp.float32),
        ),
        grid_spec=pltpu.PrefetchScalarGridSpec(
            num_scalar_prefetch=4,
            grid=(n_req, pairs),
            in_specs=[q_spec(0), kv_spec(0), q_spec(1), kv_spec(1)],
            out_specs=[
                pl.BlockSpec((1, n_query, stacked, HD), lambda r, k, rw, pk, vd, wh: (r, 0, 0, 0)),
                pl.BlockSpec((1, n_query, heads, QLEN), lambda r, k, rw, pk, vd, wh: (r, 0, 0, 0)),
                pl.BlockSpec((1, n_query, heads, QLEN), lambda r, k, rw, pk, vd, wh: (r, 0, 0, 0)),
            ],
            scratch_shapes=[
                pltpu.VMEM((n_query, stacked, HD), jnp.float32),
                pltpu.VMEM((n_query, stacked, 1), jnp.float32),
                pltpu.VMEM((n_query, stacked, 1), jnp.float32),
            ],
        ),
        cost_estimate=pl.CostEstimate(
            flops=flops,
            transcendentals=n_slots * heads * QLEN * PLEN,
            bytes_accessed=n_slots * (QLEN * width * 2 + PLEN * 2 * HD * 2)
            + n_req * n_query * stacked * HD * 2,
        ),
    )(rows, pick, valid, which, q_blocks, store, q_blocks, store)


def own_part(query_rows, own_rows):
    count, tokens, width = query_rows.shape
    heads = width // HD
    q = query_rows.reshape(count, tokens, heads, HD)
    keys = own_rows[:, :, 0:HD]
    values = own_rows[:, :, HD:2 * HD]
    s = jnp.einsum("qthd,qld->qhtl", q, keys, preferred_element_type=jnp.float32) / math.sqrt(HD)
    visible = jnp.arange(tokens)[None, :] <= jnp.arange(tokens)[:, None]
    s = jnp.where(visible, s, -jnp.inf)
    m = jnp.max(s, axis=-1, keepdims=True)
    p = jnp.exp(s - m)
    total = jnp.sum(p, axis=-1, keepdims=True)
    acc = jnp.einsum(
        "qhtl,qld->qhtd", p.astype(jnp.bfloat16), values, preferred_element_type=jnp.float32
    )
    return acc, m, total


def shards(queries, own_kv, passage_store, out_weight, passage_slot, retrieved):
    n_cache = lax.axis_size("cache")
    store_count = passage_store.shape[0]
    slot_total = passage_slot.shape[0]
    query_count, per_query = retrieved.shape
    width = queries.shape[1]
    heads = width // HD
    wanted_count = query_count * per_query
    capacity = max(2, (2 * wanted_count + n_cache - 1) // n_cache)
    capacity += capacity % 2
    wanted = retrieved.reshape(wanted_count)
    id_match = wanted[:, None] == jnp.arange(slot_total, dtype=jnp.int32)[None, :]
    store_slots = jnp.sum(jnp.where(id_match, passage_slot[None, :], 0), axis=1)
    owners = store_slots // store_count
    local_rows = store_slots % store_count
    places = jnp.arange(wanted_count, dtype=jnp.int32)
    earlier = (owners[None, :] == owners[:, None]) & (places[None, :] < places[:, None])
    order_rank = jnp.sum(earlier, axis=1)
    flat_slot = owners * capacity + order_rank
    slot_match = flat_slot[:, None] == jnp.arange(n_cache * capacity, dtype=jnp.int32)[None, :]
    send_rows = jnp.sum(jnp.where(slot_match, local_rows[:, None], 0), axis=0)
    send_query = jnp.sum(jnp.where(slot_match, (places // per_query)[:, None], 0), axis=0)
    send_valid = jnp.sum(slot_match.astype(jnp.int32), axis=0)
    info = jnp.stack([send_rows, send_query, send_valid], axis=0).reshape(3, n_cache, capacity)
    asked = lax.all_to_all(info, "cache", split_axis=1, concat_axis=1, tiled=True)
    asked_rows = asked[0].reshape(n_cache * capacity)
    asked_query = asked[1]
    requester = jnp.arange(n_cache, dtype=jnp.int32)[:, None]
    pick = (requester * query_count + asked_query).reshape(n_cache * capacity)

    everyone_q = lax.all_gather(queries, "cache", axis=0, tiled=True)
    q_blocks = everyone_q.reshape(n_cache * query_count, QLEN, width)
    merged_acc, merged_peak, merged_total = slot_attention(
        asked_rows, pick, asked[2].reshape(n_cache * capacity), asked_query.reshape(n_cache * capacity),
        q_blocks, passage_store, n_cache, capacity, query_count,
    )
    peak_ref = lax.reduce_precision(merged_peak, exponent_bits=8, mantissa_bits=7)
    shift = jnp.where(merged_peak > LIVE, jnp.exp(merged_peak - peak_ref), 0.0)
    sent_acc = (merged_acc.reshape(n_cache, query_count, heads, QLEN, HD) * shift[..., None]).astype(
        jnp.bfloat16
    )
    sent_total = merged_total * shift
    total_hi = lax.reduce_precision(sent_total, exponent_bits=8, mantissa_bits=7)
    total_lo = sent_total - total_hi
    stats = jnp.stack([peak_ref, total_hi, total_lo], axis=2).astype(jnp.bfloat16)
    packed = jnp.concatenate(
        [sent_acc.reshape(n_cache, query_count, heads * QLEN, HD),
         stats.reshape(n_cache, query_count, 3 * heads, QLEN)],
        axis=2,
    )
    back = lax.all_to_all(packed, "cache", split_axis=0, concat_axis=0, tiled=True)
    back_acc = back[:, :, :heads * QLEN].reshape(n_cache, query_count, heads, QLEN, HD)
    back_stats = back[:, :, heads * QLEN:].astype(jnp.float32).reshape(
        n_cache, query_count, 3, heads, QLEN
    )

    own_acc, own_peak, own_total = own_part(
        queries.reshape(query_count, QLEN, width),
        own_kv.reshape(query_count, QLEN, own_kv.shape[1]),
    )
    far_peak = back_stats[:, :, 0][..., None]
    far_total = (back_stats[:, :, 1] + back_stats[:, :, 2])[..., None]
    top = jnp.maximum(jnp.max(far_peak, axis=0), own_peak)
    far_scale = jnp.exp(far_peak - top[None])
    own_scale = jnp.exp(own_peak - top)
    numer = jnp.sum(far_scale * back_acc.astype(jnp.float32), axis=0) + own_scale * own_acc
    denom = jnp.sum(far_scale * far_total, axis=0) + own_scale * own_total
    attended = (numer / denom).astype(jnp.bfloat16)
    attended = jnp.transpose(attended, (0, 2, 1, 3)).reshape(query_count * QLEN, width)
    return project(attended, out_weight)


def project(attended, out_weight):
    n_cache = lax.axis_size("cache")
    n_stream = lax.axis_size("stream")
    rows = attended.shape[0]
    group = n_cache // n_stream
    everyone = lax.all_gather(attended, "cache", axis=0, tiled=True)
    partial_sums = jnp.dot(everyone, out_weight, preferred_element_type=jnp.float32)
    reduced = lax.psum_scatter(
        partial_sums.astype(jnp.bfloat16), "stream", scatter_dimension=0, tiled=True
    )
    me = lax.axis_index("cache")
    width = reduced.shape[1]
    out = jnp.zeros((rows, group * width), reduced.dtype)
    for r in range(group):
        take = (me % group + r) % group
        piece = lax.dynamic_slice_in_dim(reduced, take * rows, rows, axis=0)
        perm = []
        for c in range(n_cache):
            for s in range(n_stream):
                dst_c = s * group + (c % group + r) % group
                dst_s = c // group
                perm.append((c * n_stream + s, dst_c * n_stream + dst_s))
        got = lax.ppermute(piece, ("cache", "stream"), perm)
        put = (me - r) % group
        out = lax.dynamic_update_slice_in_dim(out, got, put * width, axis=1)
    return out


def solution(mesh):
    return jax.shard_map(
        shards,
        mesh=mesh,
        in_specs=(
            P("cache", "stream"),
            P("cache", "stream"),
            P("cache", None, "stream"),
            P("stream", "cache"),
            P(),
            P("cache", None),
        ),
        out_specs=P("cache", "stream"),
        check_vma=False,
    )
```

```python
import math

import jax
import jax.numpy as jnp
from jax import lax
from jax.experimental import pallas as pl
from jax.experimental.pallas import tpu as pltpu
from jax.sharding import PartitionSpec as P

HD = 128
QLEN = 128
PLEN = 512
FLOOR = -1e30
LIVE = -1e20


def slot_kernel(rows_ref, pick_ref, valid_ref, which_ref, q0_ref, kv0_ref, q1_ref, kv1_ref,
                acc_out, peak_out, total_out, acc_sc, peak_sc, total_sc):
    r = pl.program_id(0)
    k = pl.program_id(1)
    pairs = pl.num_programs(1)
    heads = q0_ref.shape[2] // HD
    fold = math.log2(math.e) / math.sqrt(HD)

    @pl.when(k == 0)
    def _():
        acc_sc[...] = jnp.zeros_like(acc_sc)
        peak_sc[...] = jnp.full_like(peak_sc, FLOOR)
        total_sc[...] = jnp.zeros_like(total_sc)

    for half, q_ref, kv_ref in ((0, q0_ref, kv0_ref), (1, q1_ref, kv1_ref)):
        i = (r * pairs + k) * 2 + half

        @pl.when(valid_ref[i] > 0)
        def _():
            j = which_ref[i]
            keys = kv_ref[0, :, 0:HD]
            values = kv_ref[0, :, HD:2 * HD]
            q = jnp.concatenate([q_ref[0, :, h * HD:(h + 1) * HD] for h in range(heads)], axis=0)
            s = lax.dot_general(
                q, keys, (((1,), (1,)), ((), ())), preferred_element_type=jnp.float32
            )
            old = peak_sc[j]
            new = jnp.maximum(old, jnp.max(s, axis=1, keepdims=True))
            fade = jnp.exp2((old - new) * fold)
            p = jnp.exp2((s - new) * fold)
            total_sc[j] = fade * total_sc[j] + jnp.sum(p, axis=1, keepdims=True)
            acc_sc[j] = fade * acc_sc[j] + jnp.dot(
                p.astype(jnp.bfloat16), values, preferred_element_type=jnp.float32
            )
            peak_sc[j] = new

    @pl.when(k == pairs - 1)
    def _():
        acc_out[0] = acc_sc[...].astype(acc_out.dtype)
        eye = lax.broadcasted_iota(jnp.int32, (QLEN, QLEN), 0) == lax.broadcasted_iota(
            jnp.int32, (QLEN, QLEN), 1
        )
        for j in range(peak_sc.shape[0]):
            for h in range(heads):
                rows = pl.ds(h * QLEN, QLEN)
                peak_out[0, j, pl.ds(h, 1), :] = jnp.sum(
                    jnp.where(eye, peak_sc[j, rows, :], 0.0), axis=0, keepdims=True
                ) * (1.0 / math.sqrt(HD))
                total_out[0, j, pl.ds(h, 1), :] = jnp.sum(
                    jnp.where(eye, total_sc[j, rows, :], 0.0), axis=0, keepdims=True
                )


def slot_attention(rows, pick, valid, which, q_blocks, store, n_req, cap, n_query):
    width = q_blocks.shape[2]
    heads = width // HD
    n_slots = n_req * cap
    pairs = cap // 2
    stacked = heads * QLEN
    flops = n_slots * heads * QLEN * PLEN * HD * 4
    q_spec = lambda half: pl.BlockSpec(
        (1, QLEN, width), lambda r, k, rw, pk, vd, wh: (pk[(r * pairs + k) * 2 + half], 0, 0)
    )
    kv_spec = lambda half: pl.BlockSpec(
        (1, PLEN, 2 * HD), lambda r, k, rw, pk, vd, wh: (rw[(r * pairs + k) * 2 + half], 0, 0)
    )
    return pl.pallas_call(
        slot_kernel,
        out_shape=(
            jax.ShapeDtypeStruct((n_req, n_query, stacked, HD), jnp.float32),
            jax.ShapeDtypeStruct((n_req, n_query, heads, QLEN), jnp.float32),
            jax.ShapeDtypeStruct((n_req, n_query, heads, QLEN), jnp.float32),
        ),
        grid_spec=pltpu.PrefetchScalarGridSpec(
            num_scalar_prefetch=4,
            grid=(n_req, pairs),
            in_specs=[q_spec(0), kv_spec(0), q_spec(1), kv_spec(1)],
            out_specs=[
                pl.BlockSpec((1, n_query, stacked, HD), lambda r, k, rw, pk, vd, wh: (r, 0, 0, 0)),
                pl.BlockSpec((1, n_query, heads, QLEN), lambda r, k, rw, pk, vd, wh: (r, 0, 0, 0)),
                pl.BlockSpec((1, n_query, heads, QLEN), lambda r, k, rw, pk, vd, wh: (r, 0, 0, 0)),
            ],
            scratch_shapes=[
                pltpu.VMEM((n_query, stacked, HD), jnp.float32),
                pltpu.VMEM((n_query, stacked, 1), jnp.float32),
                pltpu.VMEM((n_query, stacked, 1), jnp.float32),
            ],
        ),
        cost_estimate=pl.CostEstimate(
            flops=flops,
            transcendentals=n_slots * heads * QLEN * PLEN,
            bytes_accessed=n_slots * (QLEN * width * 2 + PLEN * 2 * HD * 2)
            + n_req * n_query * stacked * HD * 2,
        ),
    )(rows, pick, valid, which, q_blocks, store, q_blocks, store)


def own_part(query_rows, own_rows):
    count, tokens, width = query_rows.shape
    heads = width // HD
    q = query_rows.reshape(count, tokens, heads, HD)
    keys = own_rows[:, :, 0:HD]
    values = own_rows[:, :, HD:2 * HD]
    s = jnp.einsum("qthd,qld->qhtl", q, keys, preferred_element_type=jnp.float32) / math.sqrt(HD)
    visible = jnp.arange(tokens)[None, :] <= jnp.arange(tokens)[:, None]
    s = jnp.where(visible, s, -jnp.inf)
    m = jnp.max(s, axis=-1, keepdims=True)
    p = jnp.exp(s - m)
    total = jnp.sum(p, axis=-1, keepdims=True)
    acc = jnp.einsum(
        "qhtl,qld->qhtd", p.astype(jnp.bfloat16), values, preferred_element_type=jnp.float32
    )
    return acc, m, total


def shards(queries, own_kv, passage_store, out_weight, passage_slot, retrieved):
    n_cache = lax.axis_size("cache")
    store_count = passage_store.shape[0]
    slot_total = passage_slot.shape[0]
    query_count, per_query = retrieved.shape
    width = queries.shape[1]
    heads = width // HD
    wanted_count = query_count * per_query
    capacity = max(2, (2 * wanted_count + n_cache - 1) // n_cache)
    capacity += capacity % 2
    wanted = retrieved.reshape(wanted_count)
    id_match = wanted[:, None] == jnp.arange(slot_total, dtype=jnp.int32)[None, :]
    store_slots = jnp.sum(jnp.where(id_match, passage_slot[None, :], 0), axis=1)
    owners = store_slots // store_count
    local_rows = store_slots % store_count
    places = jnp.arange(wanted_count, dtype=jnp.int32)
    earlier = (owners[None, :] == owners[:, None]) & (places[None, :] < places[:, None])
    order_rank = jnp.sum(earlier, axis=1)
    flat_slot = owners * capacity + order_rank
    slot_match = flat_slot[:, None] == jnp.arange(n_cache * capacity, dtype=jnp.int32)[None, :]
    send_rows = jnp.sum(jnp.where(slot_match, local_rows[:, None], 0), axis=0)
    send_query = jnp.sum(jnp.where(slot_match, (places // per_query)[:, None], 0), axis=0)
    send_valid = jnp.sum(slot_match.astype(jnp.int32), axis=0)
    info = jnp.stack([send_rows, send_query, send_valid], axis=0).reshape(3, n_cache, capacity)
    asked = lax.all_to_all(info, "cache", split_axis=1, concat_axis=1, tiled=True)
    asked_rows = asked[0].reshape(n_cache * capacity)
    asked_query = asked[1]
    requester = jnp.arange(n_cache, dtype=jnp.int32)[:, None]
    pick = (requester * query_count + asked_query).reshape(n_cache * capacity)

    everyone_q = lax.all_gather(queries, "cache", axis=0, tiled=True)
    q_blocks = everyone_q.reshape(n_cache * query_count, QLEN, width)
    me = lax.axis_index("cache")
    mine = lax.dynamic_index_in_dim(asked, me, axis=1, keepdims=False)
    near = slot_attention(
        mine[0], mine[1], mine[2], mine[1], queries.reshape(query_count, QLEN, width),
        passage_store, 1, capacity, query_count,
    )
    others = jnp.where(requester == me, 0, asked[2]).reshape(n_cache * capacity)
    far = slot_attention(
        asked_rows, pick, others, asked_query.reshape(n_cache * capacity),
        q_blocks, passage_store, n_cache, capacity, query_count,
    )
    merged_acc, merged_peak, merged_total = (
        lax.dynamic_update_slice_in_dim(b, a, me, axis=0) for a, b in zip(near, far)
    )
    peak_ref = lax.reduce_precision(merged_peak, exponent_bits=8, mantissa_bits=7)
    shift = jnp.where(merged_peak > LIVE, jnp.exp(merged_peak - peak_ref), 0.0)
    sent_acc = (merged_acc.reshape(n_cache, query_count, heads, QLEN, HD) * shift[..., None]).astype(
        jnp.bfloat16
    )
    sent_total = merged_total * shift
    total_hi = lax.reduce_precision(sent_total, exponent_bits=8, mantissa_bits=7)
    total_lo = sent_total - total_hi
    stats = jnp.stack([peak_ref, total_hi, total_lo], axis=2).astype(jnp.bfloat16)
    packed = jnp.concatenate(
        [sent_acc.reshape(n_cache, query_count, heads * QLEN, HD),
         stats.reshape(n_cache, query_count, 3 * heads, QLEN)],
        axis=2,
    )
    back = lax.all_to_all(packed, "cache", split_axis=0, concat_axis=0, tiled=True)
    back_acc = back[:, :, :heads * QLEN].reshape(n_cache, query_count, heads, QLEN, HD)
    back_stats = back[:, :, heads * QLEN:].astype(jnp.float32).reshape(
        n_cache, query_count, 3, heads, QLEN
    )

    own_acc, own_peak, own_total = own_part(
        queries.reshape(query_count, QLEN, width),
        own_kv.reshape(query_count, QLEN, own_kv.shape[1]),
    )
    far_peak = back_stats[:, :, 0][..., None]
    far_total = (back_stats[:, :, 1] + back_stats[:, :, 2])[..., None]
    top = jnp.maximum(jnp.max(far_peak, axis=0), own_peak)
    far_scale = jnp.exp(far_peak - top[None])
    own_scale = jnp.exp(own_peak - top)
    numer = jnp.sum(far_scale * back_acc.astype(jnp.float32), axis=0) + own_scale * own_acc
    denom = jnp.sum(far_scale * far_total, axis=0) + own_scale * own_total
    attended = (numer / denom).astype(jnp.bfloat16)
    attended = jnp.transpose(attended, (0, 2, 1, 3)).reshape(query_count * QLEN, width)
    return project(attended, out_weight)


def project(attended, out_weight):
    n_cache = lax.axis_size("cache")
    n_stream = lax.axis_size("stream")
    rows = attended.shape[0]
    group = n_cache // n_stream
    everyone = lax.all_gather(attended, "cache", axis=0, tiled=True)
    partial_sums = jnp.dot(everyone, out_weight, preferred_element_type=jnp.float32)
    reduced = lax.psum_scatter(
        partial_sums.astype(jnp.bfloat16), "stream", scatter_dimension=0, tiled=True
    )
    me = lax.axis_index("cache")
    width = reduced.shape[1]
    out = jnp.zeros((rows, group * width), reduced.dtype)
    for r in range(group):
        take = (me % group + r) % group
        piece = lax.dynamic_slice_in_dim(reduced, take * rows, rows, axis=0)
        perm = []
        for c in range(n_cache):
            for s in range(n_stream):
                dst_c = s * group + (c % group + r) % group
                dst_s = c // group
                perm.append((c * n_stream + s, dst_c * n_stream + dst_s))
        got = lax.ppermute(piece, ("cache", "stream"), perm)
        put = (me - r) % group
        out = lax.dynamic_update_slice_in_dim(out, got, put * width, axis=1)
    return out


def solution(mesh):
    return jax.shard_map(
        shards,
        mesh=mesh,
        in_specs=(
            P("cache", "stream"),
            P("cache", "stream"),
            P("cache", None, "stream"),
            P("stream", "cache"),
            P(),
            P("cache", None),
        ),
        out_specs=P("cache", "stream"),
        check_vma=False,
    )
```

```python
import math

import jax
import jax.numpy as jnp
from jax import lax
from jax.experimental import pallas as pl
from jax.experimental.pallas import tpu as pltpu
from jax.sharding import PartitionSpec as P

HD = 128
QLEN = 128
PLEN = 512
FLOOR = -1e30
LIVE = -1e20


def slot_kernel(rows_ref, pick_ref, valid_ref, which_ref, q0_ref, kv0_ref, q1_ref, kv1_ref,
                acc_out, peak_out, total_out, acc_sc, peak_sc, total_sc):
    r = pl.program_id(0)
    k = pl.program_id(1)
    pairs = pl.num_programs(1)
    heads = q0_ref.shape[2] // HD
    fold = math.log2(math.e) / math.sqrt(HD)

    @pl.when(k == 0)
    def _():
        acc_sc[...] = jnp.zeros_like(acc_sc)
        peak_sc[...] = jnp.full_like(peak_sc, FLOOR)
        total_sc[...] = jnp.zeros_like(total_sc)

    for half, q_ref, kv_ref in ((0, q0_ref, kv0_ref), (1, q1_ref, kv1_ref)):
        i = (r * pairs + k) * 2 + half

        @pl.when(valid_ref[i] > 0)
        def _():
            j = which_ref[i]
            keys = kv_ref[0, :, 0:HD]
            values = kv_ref[0, :, HD:2 * HD]
            q = jnp.concatenate([q_ref[0, :, h * HD:(h + 1) * HD] for h in range(heads)], axis=0)
            s = lax.dot_general(
                q, keys, (((1,), (1,)), ((), ())), preferred_element_type=jnp.float32
            )
            old = peak_sc[j]
            new = jnp.maximum(old, jnp.max(s, axis=1, keepdims=True))
            fade = jnp.exp2((old - new) * fold)
            p = jnp.exp2((s - new) * fold)
            total_sc[j] = fade * total_sc[j] + jnp.sum(p, axis=1, keepdims=True)
            acc_sc[j] = fade * acc_sc[j] + jnp.dot(
                p.astype(jnp.bfloat16), values, preferred_element_type=jnp.float32
            )
            peak_sc[j] = new

    @pl.when(k == pairs - 1)
    def _():
        acc_out[0] = acc_sc[...].astype(acc_out.dtype)
        eye = lax.broadcasted_iota(jnp.int32, (QLEN, QLEN), 0) == lax.broadcasted_iota(
            jnp.int32, (QLEN, QLEN), 1
        )
        for j in range(peak_sc.shape[0]):
            for h in range(heads):
                rows = pl.ds(h * QLEN, QLEN)
                peak_out[0, j, pl.ds(h, 1), :] = jnp.sum(
                    jnp.where(eye, peak_sc[j, rows, :], 0.0), axis=0, keepdims=True
                ) * (1.0 / math.sqrt(HD))
                total_out[0, j, pl.ds(h, 1), :] = jnp.sum(
                    jnp.where(eye, total_sc[j, rows, :], 0.0), axis=0, keepdims=True
                )


def slot_attention(rows, pick, valid, which, q_blocks, store, n_req, cap, n_query):
    width = q_blocks.shape[2]
    heads = width // HD
    n_slots = n_req * cap
    pairs = cap // 2
    stacked = heads * QLEN
    flops = n_slots * heads * QLEN * PLEN * HD * 4
    q_spec = lambda half: pl.BlockSpec(
        (1, QLEN, width), lambda r, k, rw, pk, vd, wh: (pk[(r * pairs + k) * 2 + half], 0, 0)
    )
    kv_spec = lambda half: pl.BlockSpec(
        (1, PLEN, 2 * HD), lambda r, k, rw, pk, vd, wh: (rw[(r * pairs + k) * 2 + half], 0, 0)
    )
    return pl.pallas_call(
        slot_kernel,
        out_shape=(
            jax.ShapeDtypeStruct((n_req, n_query, stacked, HD), jnp.float32),
            jax.ShapeDtypeStruct((n_req, n_query, heads, QLEN), jnp.float32),
            jax.ShapeDtypeStruct((n_req, n_query, heads, QLEN), jnp.float32),
        ),
        grid_spec=pltpu.PrefetchScalarGridSpec(
            num_scalar_prefetch=4,
            grid=(n_req, pairs),
            in_specs=[q_spec(0), kv_spec(0), q_spec(1), kv_spec(1)],
            out_specs=[
                pl.BlockSpec((1, n_query, stacked, HD), lambda r, k, rw, pk, vd, wh: (r, 0, 0, 0)),
                pl.BlockSpec((1, n_query, heads, QLEN), lambda r, k, rw, pk, vd, wh: (r, 0, 0, 0)),
                pl.BlockSpec((1, n_query, heads, QLEN), lambda r, k, rw, pk, vd, wh: (r, 0, 0, 0)),
            ],
            scratch_shapes=[
                pltpu.VMEM((n_query, stacked, HD), jnp.float32),
                pltpu.VMEM((n_query, stacked, 1), jnp.float32),
                pltpu.VMEM((n_query, stacked, 1), jnp.float32),
            ],
        ),
        cost_estimate=pl.CostEstimate(
            flops=flops,
            transcendentals=n_slots * heads * QLEN * PLEN,
            bytes_accessed=n_slots * (QLEN * width * 2 + PLEN * 2 * HD * 2)
            + n_req * n_query * stacked * HD * 2,
        ),
    )(rows, pick, valid, which, q_blocks, store, q_blocks, store)


def own_part(query_rows, own_rows):
    count, tokens, width = query_rows.shape
    heads = width // HD
    q = query_rows.reshape(count, tokens, heads, HD)
    keys = own_rows[:, :, 0:HD]
    values = own_rows[:, :, HD:2 * HD]
    s = jnp.einsum("qthd,qld->qhtl", q, keys, preferred_element_type=jnp.float32) / math.sqrt(HD)
    visible = jnp.arange(tokens)[None, :] <= jnp.arange(tokens)[:, None]
    s = jnp.where(visible, s, -jnp.inf)
    m = jnp.max(s, axis=-1, keepdims=True)
    p = jnp.exp(s - m)
    total = jnp.sum(p, axis=-1, keepdims=True)
    acc = jnp.einsum(
        "qhtl,qld->qhtd", p.astype(jnp.bfloat16), values, preferred_element_type=jnp.float32
    )
    return acc, m, total


def shards(queries, own_kv, passage_store, out_weight, passage_slot, retrieved):
    n_cache = lax.axis_size("cache")
    store_count = passage_store.shape[0]
    slot_total = passage_slot.shape[0]
    query_count, per_query = retrieved.shape
    width = queries.shape[1]
    heads = width // HD
    wanted_count = query_count * per_query
    capacity = max(2, (2 * wanted_count + n_cache - 1) // n_cache)
    capacity += capacity % 2
    wanted = retrieved.reshape(wanted_count)
    id_match = wanted[:, None] == jnp.arange(slot_total, dtype=jnp.int32)[None, :]
    store_slots = jnp.sum(jnp.where(id_match, passage_slot[None, :], 0), axis=1)
    owners = store_slots // store_count
    local_rows = store_slots % store_count
    places = jnp.arange(wanted_count, dtype=jnp.int32)
    earlier = (owners[None, :] == owners[:, None]) & (places[None, :] < places[:, None])
    order_rank = jnp.sum(earlier, axis=1)
    flat_slot = owners * capacity + order_rank
    slot_match = flat_slot[:, None] == jnp.arange(n_cache * capacity, dtype=jnp.int32)[None, :]
    send_rows = jnp.sum(jnp.where(slot_match, local_rows[:, None], 0), axis=0)
    send_query = jnp.sum(jnp.where(slot_match, (places // per_query)[:, None], 0), axis=0)
    send_valid = jnp.sum(slot_match.astype(jnp.int32), axis=0)
    info = jnp.stack([send_rows, send_query, send_valid], axis=0).reshape(3, n_cache, capacity)
    asked = lax.all_to_all(info, "cache", split_axis=1, concat_axis=1, tiled=True)
    asked_rows = asked[0].reshape(n_cache * capacity)
    asked_query = asked[1]
    requester = jnp.arange(n_cache, dtype=jnp.int32)[:, None]
    pick = (requester * query_count + asked_query).reshape(n_cache * capacity)

    everyone_q = lax.all_gather(queries, "cache", axis=0, tiled=True)
    q_blocks = everyone_q.reshape(n_cache * query_count, QLEN, width)
    me = lax.axis_index("cache")
    mine = lax.dynamic_index_in_dim(asked, me, axis=1, keepdims=False)
    near = slot_attention(
        mine[0], mine[1], mine[2], mine[1], queries.reshape(query_count, QLEN, width),
        passage_store, 1, capacity, query_count,
    )
    mate = me + 1 - 2 * (me % 2)
    mate_q = lax.ppermute(
        queries.reshape(query_count, QLEN, width), "cache",
        [(c, c + 1 - 2 * (c % 2)) for c in range(n_cache)],
    )
    theirs = lax.dynamic_index_in_dim(asked, mate, axis=1, keepdims=False)
    beside = slot_attention(
        theirs[0], theirs[1], theirs[2], theirs[1], mate_q,
        passage_store, 1, capacity, query_count,
    )
    skip = (requester == me) | (requester == mate)
    others = jnp.where(skip, 0, asked[2]).reshape(n_cache * capacity)
    far = slot_attention(
        asked_rows, pick, others, asked_query.reshape(n_cache * capacity),
        q_blocks, passage_store, n_cache, capacity, query_count,
    )
    merged_acc, merged_peak, merged_total = (
        lax.dynamic_update_slice_in_dim(
            lax.dynamic_update_slice_in_dim(b, a, me, axis=0), m, mate, axis=0
        )
        for a, m, b in zip(near, beside, far)
    )
    peak_ref = lax.reduce_precision(merged_peak, exponent_bits=8, mantissa_bits=7)
    shift = jnp.where(merged_peak > LIVE, jnp.exp(merged_peak - peak_ref), 0.0)
    sent_acc = (merged_acc.reshape(n_cache, query_count, heads, QLEN, HD) * shift[..., None]).astype(
        jnp.bfloat16
    )
    sent_total = merged_total * shift
    total_hi = lax.reduce_precision(sent_total, exponent_bits=8, mantissa_bits=7)
    total_lo = sent_total - total_hi
    stats = jnp.stack([peak_ref, total_hi, total_lo], axis=2).astype(jnp.bfloat16)
    packed = jnp.concatenate(
        [sent_acc.reshape(n_cache, query_count, heads * QLEN, HD),
         stats.reshape(n_cache, query_count, 3 * heads, QLEN)],
        axis=2,
    )
    back = lax.all_to_all(packed, "cache", split_axis=0, concat_axis=0, tiled=True)
    back_acc = back[:, :, :heads * QLEN].reshape(n_cache, query_count, heads, QLEN, HD)
    back_stats = back[:, :, heads * QLEN:].astype(jnp.float32).reshape(
        n_cache, query_count, 3, heads, QLEN
    )

    own_acc, own_peak, own_total = own_part(
        queries.reshape(query_count, QLEN, width),
        own_kv.reshape(query_count, QLEN, own_kv.shape[1]),
    )
    far_peak = back_stats[:, :, 0][..., None]
    far_total = (back_stats[:, :, 1] + back_stats[:, :, 2])[..., None]
    top = jnp.maximum(jnp.max(far_peak, axis=0), own_peak)
    far_scale = jnp.exp(far_peak - top[None])
    own_scale = jnp.exp(own_peak - top)
    numer = jnp.sum(far_scale * back_acc.astype(jnp.float32), axis=0) + own_scale * own_acc
    denom = jnp.sum(far_scale * far_total, axis=0) + own_scale * own_total
    attended = (numer / denom).astype(jnp.bfloat16)
    attended = jnp.transpose(attended, (0, 2, 1, 3)).reshape(query_count * QLEN, width)
    return project(attended, out_weight)


def project(attended, out_weight):
    n_cache = lax.axis_size("cache")
    n_stream = lax.axis_size("stream")
    rows = attended.shape[0]
    group = n_cache // n_stream
    everyone = lax.all_gather(attended, "cache", axis=0, tiled=True)
    partial_sums = jnp.dot(everyone, out_weight, preferred_element_type=jnp.float32)
    reduced = lax.psum_scatter(
        partial_sums.astype(jnp.bfloat16), "stream", scatter_dimension=0, tiled=True
    )
    me = lax.axis_index("cache")
    width = reduced.shape[1]
    out = jnp.zeros((rows, group * width), reduced.dtype)
    for r in range(group):
        take = (me % group + r) % group
        piece = lax.dynamic_slice_in_dim(reduced, take * rows, rows, axis=0)
        perm = []
        for c in range(n_cache):
            for s in range(n_stream):
                dst_c = s * group + (c % group + r) % group
                dst_s = c // group
                perm.append((c * n_stream + s, dst_c * n_stream + dst_s))
        got = lax.ppermute(piece, ("cache", "stream"), perm)
        put = (me - r) % group
        out = lax.dynamic_update_slice_in_dim(out, got, put * width, axis=1)
    return out


def solution(mesh):
    return jax.shard_map(
        shards,
        mesh=mesh,
        in_specs=(
            P("cache", "stream"),
            P("cache", "stream"),
            P("cache", None, "stream"),
            P("stream", "cache"),
            P(),
            P("cache", None),
        ),
        out_specs=P("cache", "stream"),
        check_vma=False,
    )
```

```python
import math

import jax
import jax.numpy as jnp
from jax import lax
from jax.experimental import pallas as pl
from jax.experimental.pallas import tpu as pltpu
from jax.sharding import PartitionSpec as P

HD = 128
QLEN = 128
PLEN = 512
FLOOR = -1e30
LIVE = -1e20


def slot_kernel(rows_ref, pick_ref, valid_ref, which_ref, q0_ref, kv0_ref, q1_ref, kv1_ref,
                acc_out, peak_out, total_out, acc_sc, peak_sc, total_sc):
    r = pl.program_id(0)
    k = pl.program_id(1)
    pairs = pl.num_programs(1)
    heads = q0_ref.shape[2] // HD
    fold = math.log2(math.e) / math.sqrt(HD)

    @pl.when(k == 0)
    def _():
        acc_sc[...] = jnp.zeros_like(acc_sc)
        peak_sc[...] = jnp.full_like(peak_sc, FLOOR)
        total_sc[...] = jnp.zeros_like(total_sc)

    for half, q_ref, kv_ref in ((0, q0_ref, kv0_ref), (1, q1_ref, kv1_ref)):
        i = (r * pairs + k) * 2 + half

        @pl.when(valid_ref[i] > 0)
        def _():
            j = which_ref[i]
            keys = kv_ref[0, :, 0:HD]
            values = kv_ref[0, :, HD:2 * HD]
            q = jnp.concatenate([q_ref[0, :, h * HD:(h + 1) * HD] for h in range(heads)], axis=0)
            s = lax.dot_general(
                q, keys, (((1,), (1,)), ((), ())), preferred_element_type=jnp.float32
            )
            old = peak_sc[j]
            new = jnp.maximum(old, jnp.max(s, axis=1, keepdims=True))
            fade = jnp.exp2((old - new) * fold)
            p = jnp.exp2((s - new) * fold)
            total_sc[j] = fade * total_sc[j] + jnp.sum(p, axis=1, keepdims=True)
            acc_sc[j] = fade * acc_sc[j] + jnp.dot(
                p.astype(jnp.bfloat16), values, preferred_element_type=jnp.float32
            )
            peak_sc[j] = new

    @pl.when(k == pairs - 1)
    def _():
        acc_out[0] = acc_sc[...].astype(acc_out.dtype)
        eye = lax.broadcasted_iota(jnp.int32, (QLEN, QLEN), 0) == lax.broadcasted_iota(
            jnp.int32, (QLEN, QLEN), 1
        )
        for j in range(peak_sc.shape[0]):
            for h in range(heads):
                rows = pl.ds(h * QLEN, QLEN)
                peak_out[0, j, pl.ds(h, 1), :] = jnp.sum(
                    jnp.where(eye, peak_sc[j, rows, :], 0.0), axis=0, keepdims=True
                ) * (1.0 / math.sqrt(HD))
                total_out[0, j, pl.ds(h, 1), :] = jnp.sum(
                    jnp.where(eye, total_sc[j, rows, :], 0.0), axis=0, keepdims=True
                )


def slot_attention(rows, pick, valid, which, q_blocks, store, n_req, cap, n_query):
    width = q_blocks.shape[2]
    heads = width // HD
    n_slots = n_req * cap
    pairs = cap // 2
    stacked = heads * QLEN
    flops = n_slots * heads * QLEN * PLEN * HD * 4
    q_spec = lambda half: pl.BlockSpec(
        (1, QLEN, width), lambda r, k, rw, pk, vd, wh: (pk[(r * pairs + k) * 2 + half], 0, 0)
    )
    kv_spec = lambda half: pl.BlockSpec(
        (1, PLEN, 2 * HD), lambda r, k, rw, pk, vd, wh: (rw[(r * pairs + k) * 2 + half], 0, 0)
    )
    return pl.pallas_call(
        slot_kernel,
        out_shape=(
            jax.ShapeDtypeStruct((n_req, n_query, stacked, HD), jnp.float32),
            jax.ShapeDtypeStruct((n_req, n_query, heads, QLEN), jnp.float32),
            jax.ShapeDtypeStruct((n_req, n_query, heads, QLEN), jnp.float32),
        ),
        grid_spec=pltpu.PrefetchScalarGridSpec(
            num_scalar_prefetch=4,
            grid=(n_req, pairs),
            in_specs=[q_spec(0), kv_spec(0), q_spec(1), kv_spec(1)],
            out_specs=[
                pl.BlockSpec((1, n_query, stacked, HD), lambda r, k, rw, pk, vd, wh: (r, 0, 0, 0)),
                pl.BlockSpec((1, n_query, heads, QLEN), lambda r, k, rw, pk, vd, wh: (r, 0, 0, 0)),
                pl.BlockSpec((1, n_query, heads, QLEN), lambda r, k, rw, pk, vd, wh: (r, 0, 0, 0)),
            ],
            scratch_shapes=[
                pltpu.VMEM((n_query, stacked, HD), jnp.float32),
                pltpu.VMEM((n_query, stacked, 1), jnp.float32),
                pltpu.VMEM((n_query, stacked, 1), jnp.float32),
            ],
        ),
        cost_estimate=pl.CostEstimate(
            flops=flops,
            transcendentals=n_slots * heads * QLEN * PLEN,
            bytes_accessed=n_slots * (QLEN * width * 2 + PLEN * 2 * HD * 2)
            + n_req * n_query * stacked * HD * 2,
        ),
    )(rows, pick, valid, which, q_blocks, store, q_blocks, store)


def own_part(query_rows, own_rows):
    count, tokens, width = query_rows.shape
    heads = width // HD
    q = query_rows.reshape(count, tokens, heads, HD)
    keys = own_rows[:, :, 0:HD]
    values = own_rows[:, :, HD:2 * HD]
    s = jnp.einsum("qthd,qld->qhtl", q, keys, preferred_element_type=jnp.float32) / math.sqrt(HD)
    visible = jnp.arange(tokens)[None, :] <= jnp.arange(tokens)[:, None]
    s = jnp.where(visible, s, -jnp.inf)
    m = jnp.max(s, axis=-1, keepdims=True)
    p = jnp.exp(s - m)
    total = jnp.sum(p, axis=-1, keepdims=True)
    acc = jnp.einsum(
        "qhtl,qld->qhtd", p.astype(jnp.bfloat16), values, preferred_element_type=jnp.float32
    )
    return acc, m, total


def shards(queries, own_kv, passage_store, out_weight, passage_slot, retrieved):
    n_cache = lax.axis_size("cache")
    store_count = passage_store.shape[0]
    slot_total = passage_slot.shape[0]
    query_count, per_query = retrieved.shape
    width = queries.shape[1]
    heads = width // HD
    wanted_count = query_count * per_query
    capacity = max(2, (2 * wanted_count + n_cache - 1) // n_cache)
    capacity += capacity % 2
    wanted = retrieved.reshape(wanted_count)
    id_match = wanted[:, None] == jnp.arange(slot_total, dtype=jnp.int32)[None, :]
    store_slots = jnp.sum(jnp.where(id_match, passage_slot[None, :], 0), axis=1)
    owners = store_slots // store_count
    local_rows = store_slots % store_count
    places = jnp.arange(wanted_count, dtype=jnp.int32)
    earlier = (owners[None, :] == owners[:, None]) & (places[None, :] < places[:, None])
    order_rank = jnp.sum(earlier, axis=1)
    flat_slot = owners * capacity + order_rank
    slot_match = flat_slot[:, None] == jnp.arange(n_cache * capacity, dtype=jnp.int32)[None, :]
    send_rows = jnp.sum(jnp.where(slot_match, local_rows[:, None], 0), axis=0)
    send_query = jnp.sum(jnp.where(slot_match, (places // per_query)[:, None], 0), axis=0)
    send_valid = jnp.sum(slot_match.astype(jnp.int32), axis=0)
    info = jnp.stack([send_rows, send_query, send_valid], axis=0).reshape(3, n_cache, capacity)
    asked = lax.all_to_all(info, "cache", split_axis=1, concat_axis=1, tiled=True)
    asked_rows = asked[0].reshape(n_cache * capacity)
    asked_query = asked[1]
    requester = jnp.arange(n_cache, dtype=jnp.int32)[:, None]
    pick = (requester * query_count + asked_query).reshape(n_cache * capacity)

    everyone_q = lax.all_gather(queries, "cache", axis=0, tiled=True)
    q_blocks = everyone_q.reshape(n_cache * query_count, QLEN, width)
    me = lax.axis_index("cache")
    mine = lax.dynamic_index_in_dim(asked, me, axis=1, keepdims=False)
    near = slot_attention(
        mine[0], mine[1], mine[2], mine[1], queries.reshape(query_count, QLEN, width),
        passage_store, 1, capacity, query_count,
    )
    early = [(me, near)]
    skip = requester == me
    for flip in (1, 2):
        mate = me + flip - 2 * (me // flip % 2) * flip
        mate_q = lax.ppermute(
            queries.reshape(query_count, QLEN, width), "cache",
            [(c, c + flip - 2 * (c // flip % 2) * flip) for c in range(n_cache)],
        )
        theirs = lax.dynamic_index_in_dim(asked, mate, axis=1, keepdims=False)
        early.append((mate, slot_attention(
            theirs[0], theirs[1], theirs[2], theirs[1], mate_q,
            passage_store, 1, capacity, query_count,
        )))
        skip = skip | (requester == mate)
    others = jnp.where(skip, 0, asked[2]).reshape(n_cache * capacity)
    far = slot_attention(
        asked_rows, pick, others, asked_query.reshape(n_cache * capacity),
        q_blocks, passage_store, n_cache, capacity, query_count,
    )
    merged = list(far)
    for at, part in early:
        merged = [lax.dynamic_update_slice_in_dim(b, a, at, axis=0) for a, b in zip(part, merged)]
    merged_acc, merged_peak, merged_total = merged
    peak_ref = lax.reduce_precision(merged_peak, exponent_bits=8, mantissa_bits=7)
    shift = jnp.where(merged_peak > LIVE, jnp.exp(merged_peak - peak_ref), 0.0)
    sent_acc = (merged_acc.reshape(n_cache, query_count, heads, QLEN, HD) * shift[..., None]).astype(
        jnp.bfloat16
    )
    sent_total = merged_total * shift
    total_hi = lax.reduce_precision(sent_total, exponent_bits=8, mantissa_bits=7)
    total_lo = sent_total - total_hi
    stats = jnp.stack([peak_ref, total_hi, total_lo], axis=2).astype(jnp.bfloat16)
    packed = jnp.concatenate(
        [sent_acc.reshape(n_cache, query_count, heads * QLEN, HD),
         stats.reshape(n_cache, query_count, 3 * heads, QLEN)],
        axis=2,
    )
    back = lax.all_to_all(packed, "cache", split_axis=0, concat_axis=0, tiled=True)
    back_acc = back[:, :, :heads * QLEN].reshape(n_cache, query_count, heads, QLEN, HD)
    back_stats = back[:, :, heads * QLEN:].astype(jnp.float32).reshape(
        n_cache, query_count, 3, heads, QLEN
    )

    own_acc, own_peak, own_total = own_part(
        queries.reshape(query_count, QLEN, width),
        own_kv.reshape(query_count, QLEN, own_kv.shape[1]),
    )
    far_peak = back_stats[:, :, 0][..., None]
    far_total = (back_stats[:, :, 1] + back_stats[:, :, 2])[..., None]
    top = jnp.maximum(jnp.max(far_peak, axis=0), own_peak)
    far_scale = jnp.exp(far_peak - top[None])
    own_scale = jnp.exp(own_peak - top)
    numer = jnp.sum(far_scale * back_acc.astype(jnp.float32), axis=0) + own_scale * own_acc
    denom = jnp.sum(far_scale * far_total, axis=0) + own_scale * own_total
    attended = (numer / denom).astype(jnp.bfloat16)
    attended = jnp.transpose(attended, (0, 2, 1, 3)).reshape(query_count * QLEN, width)
    return project(attended, out_weight)


def project(attended, out_weight):
    n_cache = lax.axis_size("cache")
    n_stream = lax.axis_size("stream")
    rows = attended.shape[0]
    group = n_cache // n_stream
    everyone = lax.all_gather(attended, "cache", axis=0, tiled=True)
    partial_sums = jnp.dot(everyone, out_weight, preferred_element_type=jnp.float32)
    reduced = lax.psum_scatter(
        partial_sums.astype(jnp.bfloat16), "stream", scatter_dimension=0, tiled=True
    )
    me = lax.axis_index("cache")
    width = reduced.shape[1]
    out = jnp.zeros((rows, group * width), reduced.dtype)
    for r in range(group):
        take = (me % group + r) % group
        piece = lax.dynamic_slice_in_dim(reduced, take * rows, rows, axis=0)
        perm = []
        for c in range(n_cache):
            for s in range(n_stream):
                dst_c = s * group + (c % group + r) % group
                dst_s = c // group
                perm.append((c * n_stream + s, dst_c * n_stream + dst_s))
        got = lax.ppermute(piece, ("cache", "stream"), perm)
        put = (me - r) % group
        out = lax.dynamic_update_slice_in_dim(out, got, put * width, axis=1)
    return out


def solution(mesh):
    return jax.shard_map(
        shards,
        mesh=mesh,
        in_specs=(
            P("cache", "stream"),
            P("cache", "stream"),
            P("cache", None, "stream"),
            P("stream", "cache"),
            P(),
            P("cache", None),
        ),
        out_specs=P("cache", "stream"),
        check_vma=False,
    )
```

```python
import math

import jax
import jax.numpy as jnp
from jax import lax
from jax.experimental import pallas as pl
from jax.experimental.pallas import tpu as pltpu
from jax.sharding import PartitionSpec as P

HD = 128
QLEN = 128
PLEN = 512
FLOOR = -1e30
LIVE = -1e20


def slot_kernel(rows_ref, pick_ref, valid_ref, which_ref, q0_ref, kv0_ref, q1_ref, kv1_ref,
                acc_out, peak_out, total_out, acc_sc, peak_sc, total_sc):
    r = pl.program_id(0)
    k = pl.program_id(1)
    pairs = pl.num_programs(1)
    heads = q0_ref.shape[2] // HD
    fold = math.log2(math.e) / math.sqrt(HD)

    @pl.when(k == 0)
    def _():
        acc_sc[...] = jnp.zeros_like(acc_sc)
        peak_sc[...] = jnp.full_like(peak_sc, FLOOR)
        total_sc[...] = jnp.zeros_like(total_sc)

    for half, q_ref, kv_ref in ((0, q0_ref, kv0_ref), (1, q1_ref, kv1_ref)):
        i = (r * pairs + k) * 2 + half

        @pl.when(valid_ref[i] > 0)
        def _():
            j = which_ref[i]
            keys = kv_ref[0, :, 0:HD]
            values = kv_ref[0, :, HD:2 * HD]
            q = jnp.concatenate([q_ref[0, :, h * HD:(h + 1) * HD] for h in range(heads)], axis=0)
            s = lax.dot_general(
                q, keys, (((1,), (1,)), ((), ())), preferred_element_type=jnp.float32
            )
            old = peak_sc[j]
            new = jnp.maximum(old, jnp.max(s, axis=1, keepdims=True))
            fade = jnp.exp2((old - new) * fold)
            p = jnp.exp2((s - new) * fold)
            total_sc[j] = fade * total_sc[j] + jnp.sum(p, axis=1, keepdims=True)
            acc_sc[j] = fade * acc_sc[j] + jnp.dot(
                p.astype(jnp.bfloat16), values, preferred_element_type=jnp.float32
            )
            peak_sc[j] = new

    @pl.when(k == pairs - 1)
    def _():
        acc_out[0] = acc_sc[...].astype(acc_out.dtype)
        eye = lax.broadcasted_iota(jnp.int32, (QLEN, QLEN), 0) == lax.broadcasted_iota(
            jnp.int32, (QLEN, QLEN), 1
        )
        for j in range(peak_sc.shape[0]):
            for h in range(heads):
                rows = pl.ds(h * QLEN, QLEN)
                peak_out[0, j, pl.ds(h, 1), :] = jnp.sum(
                    jnp.where(eye, peak_sc[j, rows, :], 0.0), axis=0, keepdims=True
                ) * (1.0 / math.sqrt(HD))
                total_out[0, j, pl.ds(h, 1), :] = jnp.sum(
                    jnp.where(eye, total_sc[j, rows, :], 0.0), axis=0, keepdims=True
                )


def slot_attention(rows, pick, valid, which, q_blocks, store, n_req, cap, n_query):
    width = q_blocks.shape[2]
    heads = width // HD
    n_slots = n_req * cap
    pairs = cap // 2
    stacked = heads * QLEN
    flops = n_slots * heads * QLEN * PLEN * HD * 4
    q_spec = lambda half: pl.BlockSpec(
        (1, QLEN, width), lambda r, k, rw, pk, vd, wh: (pk[(r * pairs + k) * 2 + half], 0, 0)
    )
    kv_spec = lambda half: pl.BlockSpec(
        (1, PLEN, 2 * HD), lambda r, k, rw, pk, vd, wh: (rw[(r * pairs + k) * 2 + half], 0, 0)
    )
    return pl.pallas_call(
        slot_kernel,
        out_shape=(
            jax.ShapeDtypeStruct((n_req, n_query, stacked, HD), jnp.float32),
            jax.ShapeDtypeStruct((n_req, n_query, heads, QLEN), jnp.float32),
            jax.ShapeDtypeStruct((n_req, n_query, heads, QLEN), jnp.float32),
        ),
        grid_spec=pltpu.PrefetchScalarGridSpec(
            num_scalar_prefetch=4,
            grid=(n_req, pairs),
            in_specs=[q_spec(0), kv_spec(0), q_spec(1), kv_spec(1)],
            out_specs=[
                pl.BlockSpec((1, n_query, stacked, HD), lambda r, k, rw, pk, vd, wh: (r, 0, 0, 0)),
                pl.BlockSpec((1, n_query, heads, QLEN), lambda r, k, rw, pk, vd, wh: (r, 0, 0, 0)),
                pl.BlockSpec((1, n_query, heads, QLEN), lambda r, k, rw, pk, vd, wh: (r, 0, 0, 0)),
            ],
            scratch_shapes=[
                pltpu.VMEM((n_query, stacked, HD), jnp.float32),
                pltpu.VMEM((n_query, stacked, 1), jnp.float32),
                pltpu.VMEM((n_query, stacked, 1), jnp.float32),
            ],
        ),
        cost_estimate=pl.CostEstimate(
            flops=flops,
            transcendentals=n_slots * heads * QLEN * PLEN,
            bytes_accessed=n_slots * (QLEN * width * 2 + PLEN * 2 * HD * 2)
            + n_req * n_query * stacked * HD * 2,
        ),
    )(rows, pick, valid, which, q_blocks, store, q_blocks, store)


def own_part(query_rows, own_rows):
    count, tokens, width = query_rows.shape
    heads = width // HD
    q = query_rows.reshape(count, tokens, heads, HD)
    keys = own_rows[:, :, 0:HD]
    values = own_rows[:, :, HD:2 * HD]
    s = jnp.einsum("qthd,qld->qhtl", q, keys, preferred_element_type=jnp.float32) / math.sqrt(HD)
    visible = jnp.arange(tokens)[None, :] <= jnp.arange(tokens)[:, None]
    s = jnp.where(visible, s, -jnp.inf)
    m = jnp.max(s, axis=-1, keepdims=True)
    p = jnp.exp(s - m)
    total = jnp.sum(p, axis=-1, keepdims=True)
    acc = jnp.einsum(
        "qhtl,qld->qhtd", p.astype(jnp.bfloat16), values, preferred_element_type=jnp.float32
    )
    return acc, m, total


def shards(queries, own_kv, passage_store, out_weight, passage_slot, retrieved):
    n_cache = lax.axis_size("cache")
    store_count = passage_store.shape[0]
    slot_total = passage_slot.shape[0]
    query_count, per_query = retrieved.shape
    width = queries.shape[1]
    heads = width // HD
    wanted_count = query_count * per_query
    capacity = max(2, (2 * wanted_count + n_cache - 1) // n_cache)
    capacity += capacity % 2
    wanted = retrieved.reshape(wanted_count)
    id_match = wanted[:, None] == jnp.arange(slot_total, dtype=jnp.int32)[None, :]
    store_slots = jnp.sum(jnp.where(id_match, passage_slot[None, :], 0), axis=1)
    owners = store_slots // store_count
    local_rows = store_slots % store_count
    places = jnp.arange(wanted_count, dtype=jnp.int32)
    earlier = (owners[None, :] == owners[:, None]) & (places[None, :] < places[:, None])
    order_rank = jnp.sum(earlier, axis=1)
    flat_slot = owners * capacity + order_rank
    slot_match = flat_slot[:, None] == jnp.arange(n_cache * capacity, dtype=jnp.int32)[None, :]
    send_rows = jnp.sum(jnp.where(slot_match, local_rows[:, None], 0), axis=0)
    send_query = jnp.sum(jnp.where(slot_match, (places // per_query)[:, None], 0), axis=0)
    send_valid = jnp.sum(slot_match.astype(jnp.int32), axis=0)
    info = jnp.stack([send_rows, send_query, send_valid], axis=0).reshape(3, n_cache, capacity)
    asked = lax.all_to_all(info, "cache", split_axis=1, concat_axis=1, tiled=True)
    asked_rows = asked[0].reshape(n_cache * capacity)
    asked_query = asked[1]
    requester = jnp.arange(n_cache, dtype=jnp.int32)[:, None]
    pick = (requester * query_count + asked_query).reshape(n_cache * capacity)

    everyone_q = lax.all_gather(queries, "cache", axis=0, tiled=True)
    q_blocks = everyone_q.reshape(n_cache * query_count, QLEN, width)
    me = lax.axis_index("cache")
    mine = lax.dynamic_index_in_dim(asked, me, axis=1, keepdims=False)
    near = slot_attention(
        mine[0], mine[1], mine[2], mine[1], queries.reshape(query_count, QLEN, width),
        passage_store, 1, capacity, query_count,
    )
    mate = me + 1 - 2 * (me % 2)
    mate_q = lax.ppermute(
        queries.reshape(query_count, QLEN, width), "cache",
        [(c, c + 1 - 2 * (c % 2)) for c in range(n_cache)],
    )
    theirs = lax.dynamic_index_in_dim(asked, mate, axis=1, keepdims=False)
    beside = slot_attention(
        theirs[0], theirs[1], theirs[2], theirs[1], mate_q,
        passage_store, 1, capacity, query_count,
    )
    skip = (requester == me) | (requester == mate)
    others = jnp.where(skip, 0, asked[2]).reshape(n_cache * capacity)
    slots = jnp.arange(n_cache * capacity, dtype=jnp.int32)
    lead = jnp.where(others > 0, slots, slots % 2)
    lead = lax.cummax(lead.reshape(-1, 2), axis=0).reshape(-1)
    far = slot_attention(
        asked_rows[lead], pick[lead], others, asked_query.reshape(n_cache * capacity),
        q_blocks, passage_store, n_cache, capacity, query_count,
    )
    merged_acc, merged_peak, merged_total = (
        lax.dynamic_update_slice_in_dim(
            lax.dynamic_update_slice_in_dim(b, a, me, axis=0), m, mate, axis=0
        )
        for a, m, b in zip(near, beside, far)
    )
    peak_ref = lax.reduce_precision(merged_peak, exponent_bits=8, mantissa_bits=7)
    shift = jnp.where(merged_peak > LIVE, jnp.exp(merged_peak - peak_ref), 0.0)
    sent_acc = (merged_acc.reshape(n_cache, query_count, heads, QLEN, HD) * shift[..., None]).astype(
        jnp.bfloat16
    )
    sent_total = merged_total * shift
    total_hi = lax.reduce_precision(sent_total, exponent_bits=8, mantissa_bits=7)
    total_lo = sent_total - total_hi
    stats = jnp.stack([peak_ref, total_hi, total_lo], axis=2).astype(jnp.bfloat16)
    packed = jnp.concatenate(
        [sent_acc.reshape(n_cache, query_count, heads * QLEN, HD),
         stats.reshape(n_cache, query_count, 3 * heads, QLEN)],
        axis=2,
    )
    back = lax.all_to_all(packed, "cache", split_axis=0, concat_axis=0, tiled=True)
    back_acc = back[:, :, :heads * QLEN].reshape(n_cache, query_count, heads, QLEN, HD)
    back_stats = back[:, :, heads * QLEN:].astype(jnp.float32).reshape(
        n_cache, query_count, 3, heads, QLEN
    )

    own_acc, own_peak, own_total = own_part(
        queries.reshape(query_count, QLEN, width),
        own_kv.reshape(query_count, QLEN, own_kv.shape[1]),
    )
    far_peak = back_stats[:, :, 0][..., None]
    far_total = (back_stats[:, :, 1] + back_stats[:, :, 2])[..., None]
    top = jnp.maximum(jnp.max(far_peak, axis=0), own_peak)
    far_scale = jnp.exp(far_peak - top[None])
    own_scale = jnp.exp(own_peak - top)
    numer = jnp.sum(far_scale * back_acc.astype(jnp.float32), axis=0) + own_scale * own_acc
    denom = jnp.sum(far_scale * far_total, axis=0) + own_scale * own_total
    attended = (numer / denom).astype(jnp.bfloat16)
    attended = jnp.transpose(attended, (0, 2, 1, 3)).reshape(query_count * QLEN, width)
    return project(attended, out_weight)


def project(attended, out_weight):
    n_cache = lax.axis_size("cache")
    n_stream = lax.axis_size("stream")
    rows = attended.shape[0]
    group = n_cache // n_stream
    everyone = lax.all_gather(attended, "cache", axis=0, tiled=True)
    partial_sums = jnp.dot(everyone, out_weight, preferred_element_type=jnp.float32)
    reduced = lax.psum_scatter(
        partial_sums.astype(jnp.bfloat16), "stream", scatter_dimension=0, tiled=True
    )
    me = lax.axis_index("cache")
    width = reduced.shape[1]
    out = jnp.zeros((rows, group * width), reduced.dtype)
    for r in range(group):
        take = (me % group + r) % group
        piece = lax.dynamic_slice_in_dim(reduced, take * rows, rows, axis=0)
        perm = []
        for c in range(n_cache):
            for s in range(n_stream):
                dst_c = s * group + (c % group + r) % group
                dst_s = c // group
                perm.append((c * n_stream + s, dst_c * n_stream + dst_s))
        got = lax.ppermute(piece, ("cache", "stream"), perm)
        put = (me - r) % group
        out = lax.dynamic_update_slice_in_dim(out, got, put * width, axis=1)
    return out


def solution(mesh):
    return jax.shard_map(
        shards,
        mesh=mesh,
        in_specs=(
            P("cache", "stream"),
            P("cache", "stream"),
            P("cache", None, "stream"),
            P("stream", "cache"),
            P(),
            P("cache", None),
        ),
        out_specs=P("cache", "stream"),
        check_vma=False,
    )
```
